512 devices in a mesh: frames: 64 (over x, y, core), tex: 8 (over z).
Axes of the slice: x: 4, y: 8, z: 8, core: 2. Of those that a mesh axis runs over, the one named last changes fastest.
Arguments:
- texture: bfloat16 [512, 16384], P('tex'), may hold values from -6 to 6
- requests: int32 [512, 32], P(('frames', 'tex')), may hold values from 0 to 63, as said below
- block_slot: int32 [512, 32], P(('frames', 'tex')), may hold values from 0 to 31
- texel_cell: int32 [512, 4096], P(('frames', 'tex')), may hold values from 0 to 960
- uv_frac: float32 [512, 2, 4096], P(('frames', 'tex')), may hold values from 0 to 1
- conv_weight: bfloat16 [32, 144], replicated, may hold values from -0.5 to 0.5
- cotangent: bfloat16 [512, 32, 4096], P(('frames', 'tex')), may hold values from -6 to 6
Outputs:
- rendered: bfloat16 [512, 32, 4096], P(('frames', 'tex'))
- texture_grad: float32 [512, 16384], P('tex', 'frames')
- weight_grad: float32 [32, 144], replicated
The draws below stay inside these ranges and needn't reach their ends.
Inputs may be any that keep to these rules, and one draw needn't show every extreme that they name: The 4 tile numbers one renderer requests from one owner are distinct.
All inputs are finite; a program needn't handle non-finite values.
Results may differ from the reference program's by a relative error of at most 0.007.
Values may be sent and summed in bfloat16 or wider, within the bound.
No kernel may reach another device: no remote copies, remote signals or barrier semaphores. Data moves between devices by JAX's collectives and lax.ppermute only.
A program may use at most 64 MiB of HBM per device.

```python
import math
import jax
import jax.numpy as jnp
from jax import lax

CH = 16
CONV = 32
TSIDE = 32
BLOCK = 128
CAP = 4
CROP_H = 32
TILE_DEV = 64
TEXEL = 1024
PIX = 4096
VIS = 32
TILES = 512
RENDERERS = 512
N_FRAMES = 64
N_TEX = 8


def draw_requests(key, part):
    count = N_FRAMES * N_TEX * N_TEX
    keys = jax.random.split(key, count)
    selected_entries = jax.vmap(lambda single: jax.random.permutation(single, TILE_DEV)[:CAP])(keys)
    return selected_entries.reshape(N_FRAMES * N_TEX, N_TEX * CAP).astype(jnp.int32)


def plant(entries, key, least, high):
    longest = entries.shape.index(max(entries.shape))
    spots = []
    for shift in (0, 1):
        where = [jax.random.randint(jax.random.fold_in(key, axis), (), 0, length) for axis, length in enumerate(entries.shape)]
        where[longest] = (where[longest] + shift) % entries.shape[longest]
        spots.append(tuple(where))
    return entries.at[spots[0]].set(least).at[spots[1]].set(high)


def shard_levels(rng, dims, pieces, low, top_value):
    loudness, own = 1.0, jax.random.fold_in(rng, 6)
    for dim, blocks in pieces:
        heights = jnp.exp(jax.random.uniform(jax.random.fold_in(own, dim), (blocks,), jnp.float32, low / len(pieces), top_value / len(pieces)))
        loudness = loudness * jnp.repeat(heights, dims[dim] // blocks).reshape([-1 if axis == dim else 1 for axis in range(len(dims))])
    return loudness


def gaussian(rng, shape, scale, most, cuts=(), kind=jnp.bfloat16):
    entries = jax.random.normal(rng, shape, jnp.float32) * scale
    if len(cuts) > 0:
        entries = shard_levels(rng, shape, cuts, -0.22, 0.18) * entries
    return jnp.clip(entries, min=-most, max=most).astype(kind)


def setup_inputs(seed: int = 0) -> dict:
    key_of = jax.random.split(jax.random.key(seed), 8)
    texture = gaussian(key_of[0], (TILES, CH * TEXEL), 1.0, 6.0, ((0, 8),))
    requests = draw_requests(jax.random.fold_in(key_of[7], 71), 0)
    block_slot = plant(jax.random.randint(key_of[2], (RENDERERS, CROP_H), 0, VIS), jax.random.fold_in(key_of[2], 1), 0, VIS - 1).astype(jnp.int32)
    texel_cell = plant(jax.random.randint(key_of[3], (RENDERERS, PIX), 0, (TSIDE - 1) * (TSIDE - 1)), jax.random.fold_in(key_of[3], 1), 0, ((TSIDE - 1) * (TSIDE - 1)) - 1).astype(jnp.int32)
    uv_frac = jnp.clip(1.0 * jax.random.uniform(key_of[4], (RENDERERS, 2, PIX), jnp.float32) ** shard_levels(key_of[4], (RENDERERS, 2, PIX), ((0, 512),), -0.2, 0.2), 0.0, 1.0)
    conv_weight = gaussian(key_of[5], (CONV, 9 * CH), (9 * CH) ** -0.5, 0.5)
    cotangent = gaussian(key_of[6], (RENDERERS, CONV, PIX), 1.0, 6.0, ((0, 512),))
    return dict(texture=texture, requests=requests, block_slot=block_slot, texel_cell=texel_cell, uv_frac=uv_frac, conv_weight=conv_weight, cotangent=cotangent)


def taps_and_weights(cell_row, frac_row, side):
    column = cell_row % (side - 1)
    row_index = cell_row // (side - 1)
    corner = (row_index * side + column).astype(jnp.int32)
    texel_taps = jnp.stack([corner, corner + 1, corner + side, corner + side + 1])
    frac_x = frac_row[0]
    frac_y = frac_row[1]
    weights = jnp.stack([(1.0 - frac_x) * (1.0 - frac_y), frac_x * (1.0 - frac_y), (1.0 - frac_x) * frac_y, frac_x * frac_y])
    return (texel_taps, weights)

def sample_matrix(texel_taps, weights, texel):
    positions = lax.broadcasted_iota(jnp.int32, (texel_taps.shape[1], texel), 1)
    matrix = jnp.zeros((texel_taps.shape[1], texel), jnp.float32)
    for number in range(4):
        matrix = matrix + jnp.where(texel_taps[number][:, None] == positions, weights[number][:, None], jnp.float32(0.0))
    return matrix.astype(jnp.bfloat16)

def shifted(picture, shift_y, shift_x):
    height = picture.shape[1]
    width = picture.shape[2]
    padded_input = jnp.pad(picture, ((0, 0), (1, 1), (1, 1)))
    return padded_input[:, 1 + shift_y:1 + shift_y + height, 1 + shift_x:1 + shift_x + width]

def render_one(fetched, slot_row, cell_row, frac_row, conv_weight, cot_row):
    visible = fetched.shape[0]
    channels = fetched.shape[1]
    texel = fetched.shape[2]
    side = math.isqrt(texel)
    height = slot_row.shape[0]
    width = cell_row.shape[0] // height
    group_size = math.gcd(height, 16)
    group_count = height // group_size
    texel_taps, weights = taps_and_weights(cell_row, frac_row, side)
    taps_grouped = texel_taps.reshape(4, group_count, group_size * width).transpose(1, 0, 2)
    weights_grouped = weights.reshape(4, group_count, group_size * width).transpose(1, 0, 2)
    slots_grouped = slot_row.reshape(group_count, group_size)

    def forward(inputs):
        taps_part, weights_part, slots_part = inputs
        texture_lookup = sample_matrix(taps_part, weights_part, texel).reshape(group_size, width, texel)
        selected_entries = jnp.take(fetched, slots_part, axis=0)
        feature_maps = jnp.einsum('qfm,qzm->qfz', selected_entries, texture_lookup, preferred_element_type=jnp.float32)
        return feature_maps.astype(jnp.bfloat16)
    grouped_features = lax.map(forward, (taps_grouped, weights_grouped, slots_grouped))
    feature_maps = grouped_features.transpose(2, 0, 1, 3).reshape(channels, height, width)
    offsets = [(shift_y, shift_x) for shift_y in (-1, 0, 1) for shift_x in (-1, 0, 1)]
    columns = jnp.concatenate([shifted(feature_maps, shift_y, shift_x) for shift_y, shift_x in offsets], axis=0)
    columns = columns.reshape(9 * channels, height * width)
    preact = jnp.dot(conv_weight, columns, preferred_element_type=jnp.float32)
    sigmoid_pre = jax.nn.sigmoid(preact)
    rendered = (preact * sigmoid_pre).astype(jnp.bfloat16)
    pre_grad = (cot_row.astype(jnp.float32) * sigmoid_pre * (1.0 + preact * (1.0 - sigmoid_pre))).astype(jnp.bfloat16)
    weight_local = jnp.einsum('op,kp->ok', pre_grad, columns, preferred_element_type=jnp.float32)
    col_grad = jnp.einsum('ok,op->kp', conv_weight, pre_grad, preferred_element_type=jnp.float32)
    col_grad = col_grad.reshape(9, channels, height, width)
    feat_grad = jnp.zeros((channels, height, width), jnp.float32)
    for number in range(9):
        shift_y, shift_x = offsets[number]
        feat_grad = feat_grad + shifted(col_grad[number], -shift_y, -shift_x)
    feat_grad = feat_grad.astype(jnp.bfloat16)
    grad_grouped = feat_grad.reshape(channels, group_count, group_size, width).transpose(1, 2, 0, 3)
    slot_numbers = jnp.arange(visible, dtype=jnp.int32)

    def backward(totals, inputs):
        taps_part, weights_part, slots_part, gradient_portion = inputs
        texture_lookup = sample_matrix(taps_part, weights_part, texel).reshape(group_size, width, texel)
        texel_gradient = jnp.einsum('rzs,rsu->rzu', gradient_portion, texture_lookup, preferred_element_type=jnp.float32)
        selector = (slots_part[:, None] == slot_numbers[None, :]).astype(jnp.float32)
        added = jnp.einsum('gv,gct->vct', selector, texel_gradient, precision=lax.Precision.HIGHEST)
        return (totals + added, None)
    start = jnp.zeros((visible, channels, texel), jnp.float32)
    slot_grad, unused = lax.scan(backward, start, (taps_grouped, weights_grouped, slots_grouped, grad_grouped))
    return (rendered, slot_grad.reshape(visible, channels * texel), weight_local)

def reference(texture, requests, block_slot, texel_cell, uv_frac, conv_weight, cotangent):
    visible = N_TEX * CAP
    render_workers = N_FRAMES * N_TEX
    owner_base = (jnp.arange(visible, dtype=jnp.int32) // CAP * TILE_DEV).astype(jnp.int32)

    def step(totals, inputs):
        tex_total, weight_total = totals
        request_row, slot_row, cell_row, frac_row, cot_row = inputs
        tile_rows = (owner_base + request_row).astype(jnp.int32)
        fetched = jnp.take(texture, tile_rows, axis=0).reshape(visible, CH, TEXEL)
        rendered, slot_grad, weight_local = render_one(fetched, slot_row, cell_row, frac_row, conv_weight, cot_row)
        tex_total = tex_total.at[tile_rows].add(slot_grad)
        return ((tex_total, weight_total + weight_local), rendered)
    start = (jnp.zeros((TILE_DEV * N_TEX, CH * TEXEL), jnp.float32), jnp.zeros((CONV, 9 * CH), jnp.float32))
    totals, rendered = lax.scan(step, start, (requests, block_slot, texel_cell, uv_frac, cotangent))
    norm_scale = 1.0 / math.sqrt(render_workers * CROP_H * BLOCK)
    return (rendered, totals[0], totals[1] * norm_scale)
```

```python
import math

import jax
import jax.numpy as jnp
from jax import lax
from jax.sharding import PartitionSpec as P

CH = 16


def taps_and_weights(cell_row, frac_row, side):
    column = cell_row % (side - 1)
    row_index = cell_row // (side - 1)
    corner = row_index * side + column
    texel_taps = jnp.stack([corner, corner + 1, corner + side, corner + side + 1])
    frac_x = frac_row[0]
    frac_y = frac_row[1]
    weights = jnp.stack(
        [
            (1.0 - frac_x) * (1.0 - frac_y),
            frac_x * (1.0 - frac_y),
            (1.0 - frac_x) * frac_y,
            frac_x * frac_y,
        ]
    )
    return (texel_taps, weights)


def sample_matrix(texel_taps, weights, texel):
    positions = lax.broadcasted_iota(jnp.int32, (texel_taps.shape[1], texel), 1)
    matrix = jnp.zeros((texel_taps.shape[1], texel), jnp.float32)
    for number in range(4):
        matrix = matrix + jnp.where(
            texel_taps[number][:, None] == positions, weights[number][:, None], jnp.float32(0.0)
        )
    return matrix.astype(jnp.bfloat16)


def shifted(picture, shift_y, shift_x):
    height = picture.shape[1]
    width = picture.shape[2]
    padded_input = jnp.pad(picture, ((0, 0), (1, 1), (1, 1)))
    return padded_input[:, 1 + shift_y : 1 + shift_y + height, 1 + shift_x : 1 + shift_x + width]


def render_one(fetched, slot_row, cell_row, frac_row, conv_weight, cot_row):
    visible = fetched.shape[0]
    channels = fetched.shape[1]
    texel = fetched.shape[2]
    side = math.isqrt(texel)
    height = slot_row.shape[0]
    width = cell_row.shape[0] // height
    group_size = math.gcd(height, 16)
    group_count = height // group_size
    texel_taps, weights = taps_and_weights(cell_row, frac_row, side)
    taps_grouped = texel_taps.reshape(4, group_count, group_size * width).transpose(1, 0, 2)
    weights_grouped = weights.reshape(4, group_count, group_size * width).transpose(1, 0, 2)
    slots_grouped = slot_row.reshape(group_count, group_size)

    def forward(inputs):
        taps_part, weights_part, slots_part = inputs
        texture_lookup = sample_matrix(taps_part, weights_part, texel).reshape(
            group_size, width, texel
        )
        selected_entries = jnp.take(fetched, slots_part, axis=0)
        feature_maps = jnp.einsum(
            "qfm,qzm->qfz", selected_entries, texture_lookup, preferred_element_type=jnp.float32
        )
        return feature_maps.astype(jnp.bfloat16)

    grouped_features = lax.map(forward, (taps_grouped, weights_grouped, slots_grouped))
    feature_maps = grouped_features.transpose(2, 0, 1, 3).reshape(channels, height, width)
    offsets = [(shift_y, shift_x) for shift_y in (-1, 0, 1) for shift_x in (-1, 0, 1)]
    columns = jnp.concatenate(
        [shifted(feature_maps, shift_y, shift_x) for shift_y, shift_x in offsets], axis=0
    )
    columns = columns.reshape(9 * channels, height * width)
    preact = jnp.dot(conv_weight, columns, preferred_element_type=jnp.float32)
    sigmoid_pre = jax.nn.sigmoid(preact)
    rendered = (preact * sigmoid_pre).astype(jnp.bfloat16)
    pre_grad = (
        cot_row.astype(jnp.float32) * sigmoid_pre * (1.0 + preact * (1.0 - sigmoid_pre))
    ).astype(jnp.bfloat16)
    weight_local = jnp.einsum("op,kp->ok", pre_grad, columns, preferred_element_type=jnp.float32)
    col_grad = jnp.einsum("ok,op->kp", conv_weight, pre_grad, preferred_element_type=jnp.float32)
    col_grad = col_grad.reshape(9, channels, height, width)
    feat_grad = jnp.zeros((channels, height, width), jnp.float32)
    for number in range(9):
        shift_y, shift_x = offsets[number]
        feat_grad = feat_grad + shifted(col_grad[number], -shift_y, -shift_x)
    feat_grad = feat_grad.astype(jnp.bfloat16)
    grad_grouped = feat_grad.reshape(channels, group_count, group_size, width).transpose(1, 2, 0, 3)
    slot_numbers = jnp.arange(visible, dtype=jnp.int32)

    def backward(totals, inputs):
        taps_part, weights_part, slots_part, gradient_portion = inputs
        texture_lookup = sample_matrix(taps_part, weights_part, texel).reshape(
            group_size, width, texel
        )
        texel_gradient = jnp.einsum(
            "rzs,rsu->rzu", gradient_portion, texture_lookup, preferred_element_type=jnp.float32
        )
        selector = (slots_part[:, None] == slot_numbers[None, :]).astype(jnp.float32)
        added = jnp.einsum("gv,gct->vct", selector, texel_gradient, precision=lax.Precision.HIGHEST)
        return (totals + added, None)

    start = jnp.zeros((visible, channels, texel), jnp.float32)
    slot_grad, unused = lax.scan(
        backward, start, (taps_grouped, weights_grouped, slots_grouped, grad_grouped)
    )
    return (rendered, slot_grad.reshape(visible, channels * texel), weight_local)


def per_device(texture, requests, block_slot, texel_cell, uv_frac, conv_weight, cotangent):
    owners = lax.axis_size("tex")
    frame_count = lax.axis_size("frames")
    tile_count = texture.shape[0]
    tile_width = texture.shape[1]
    wanted_ids = requests.reshape(owners, -1)
    wanted = lax.all_to_all(wanted_ids, "tex", split_axis=0, concat_axis=0, tiled=True)
    served = jnp.take(texture, wanted.reshape(-1), axis=0).reshape(
        wanted.shape[0], wanted.shape[1], tile_width
    )
    returned_tiles = lax.all_to_all(served, "tex", split_axis=0, concat_axis=0, tiled=True)
    fetched = returned_tiles
    per_owner = fetched.shape[1]
    visible = owners * per_owner
    fetched = fetched.reshape(visible, CH, tile_width // CH)
    rendered, slot_grad, weight_local = render_one(
        fetched, block_slot[0], texel_cell[0], uv_frac[0], conv_weight, cotangent[0]
    )
    columns = tile_width // frame_count
    spread = slot_grad.reshape(visible, frame_count, columns).transpose(1, 0, 2)
    gathered = lax.all_to_all(spread, "frames", split_axis=0, concat_axis=0, tiled=True)
    gathered = gathered.reshape(frame_count, owners, per_owner, columns)
    senders = lax.all_gather(requests[0], "frames").reshape(frame_count, owners, per_owner)
    tile_numbers = jnp.arange(tile_count, dtype=jnp.int32)
    selector = (senders[None] == tile_numbers[:, None, None, None]).astype(jnp.float32)
    partial = jnp.einsum(
        "qfoj,fojc->oqc", selector, gathered, precision=lax.Precision.HIGHEST
    )
    texture_grad = lax.psum_scatter(partial, "tex", scatter_dimension=0, tiled=True)
    texture_grad = texture_grad.reshape(tile_count, columns)
    norm_scale = 1.0 / math.sqrt(frame_count * owners * cotangent.shape[2])
    weight_grad = lax.psum(weight_local, ("frames", "tex")) * norm_scale
    return (rendered[None], texture_grad, weight_grad)


def solution(mesh):
    placed = (
        P("tex", None),
        P(("frames", "tex"), None),
        P(("frames", "tex"), None),
        P(("frames", "tex"), None),
        P(("frames", "tex"), None, None),
        P(),
        P(("frames", "tex"), None, None),
    )
    return jax.shard_map(
        per_device,
        mesh=mesh,
        in_specs=placed,
        out_specs=(P(("frames", "tex"), None, None), P("tex", "frames"), P()),
        check_vma=False,
    )
```

```python
import math

import jax
import jax.numpy as jnp
from jax import lax
from jax.sharding import PartitionSpec as P

CH = 16


def taps_and_weights(cell_row, frac_row, side):
    column = cell_row % (side - 1)
    row_index = cell_row // (side - 1)
    corner = row_index * side + column
    texel_taps = jnp.stack([corner, corner + 1, corner + side, corner + side + 1])
    frac_x = frac_row[0]
    frac_y = frac_row[1]
    weights = jnp.stack(
        [
            (1.0 - frac_x) * (1.0 - frac_y),
            frac_x * (1.0 - frac_y),
            (1.0 - frac_x) * frac_y,
            frac_x * frac_y,
        ]
    )
    return (texel_taps, weights)


def sample_matrix(texel_taps, weights, texel):
    positions = lax.broadcasted_iota(jnp.int32, (texel_taps.shape[1], texel), 1)
    matrix = jnp.zeros((texel_taps.shape[1], texel), jnp.float32)
    for number in range(4):
        matrix = matrix + jnp.where(
            texel_taps[number][:, None] == positions, weights[number][:, None], jnp.float32(0.0)
        )
    return matrix.astype(jnp.bfloat16)


def shifted(picture, shift_y, shift_x):
    height = picture.shape[1]
    width = picture.shape[2]
    padded_input = jnp.pad(picture, ((0, 0), (1, 1), (1, 1)))
    return padded_input[:, 1 + shift_y : 1 + shift_y + height, 1 + shift_x : 1 + shift_x + width]


def render_one(fetched, slot_row, cell_row, frac_row, conv_weight, cot_row):
    visible = fetched.shape[0]
    channels = fetched.shape[1]
    texel = fetched.shape[2]
    side = math.isqrt(texel)
    height = slot_row.shape[0]
    width = cell_row.shape[0] // height
    group_size = math.gcd(height, 16)
    group_count = height // group_size
    texel_taps, weights = taps_and_weights(cell_row, frac_row, side)
    taps_grouped = texel_taps.reshape(4, group_count, group_size * width).transpose(1, 0, 2)
    weights_grouped = weights.reshape(4, group_count, group_size * width).transpose(1, 0, 2)
    slots_grouped = slot_row.reshape(group_count, group_size)

    def forward(inputs):
        taps_part, weights_part, slots_part = inputs
        texture_lookup = sample_matrix(taps_part, weights_part, texel).reshape(
            group_size, width, texel
        )
        selected_entries = jnp.take(fetched, slots_part, axis=0)
        feature_maps = jnp.einsum(
            "qfm,qzm->qfz", selected_entries, texture_lookup, preferred_element_type=jnp.float32
        )
        return feature_maps.astype(jnp.bfloat16)

    grouped_features = lax.map(forward, (taps_grouped, weights_grouped, slots_grouped))
    feature_maps = grouped_features.transpose(2, 0, 1, 3).reshape(channels, height, width)
    offsets = [(shift_y, shift_x) for shift_y in (-1, 0, 1) for shift_x in (-1, 0, 1)]
    columns = jnp.concatenate(
        [shifted(feature_maps, shift_y, shift_x) for shift_y, shift_x in offsets], axis=0
    )
    columns = columns.reshape(9 * channels, height * width)
    preact = jnp.dot(conv_weight, columns, preferred_element_type=jnp.float32)
    sigmoid_pre = jax.nn.sigmoid(preact)
    rendered = (preact * sigmoid_pre).astype(jnp.bfloat16)
    pre_grad = (
        cot_row.astype(jnp.float32) * sigmoid_pre * (1.0 + preact * (1.0 - sigmoid_pre))
    ).astype(jnp.bfloat16)
    weight_local = jnp.einsum("op,kp->ok", pre_grad, columns, preferred_element_type=jnp.float32)
    col_grad = jnp.einsum("ok,op->kp", conv_weight, pre_grad, preferred_element_type=jnp.float32)
    col_grad = col_grad.reshape(9, channels, height, width)
    feat_grad = jnp.zeros((channels, height, width), jnp.float32)
    for number in range(9):
        shift_y, shift_x = offsets[number]
        feat_grad = feat_grad + shifted(col_grad[number], -shift_y, -shift_x)
    feat_grad = feat_grad.astype(jnp.bfloat16)
    grad_grouped = feat_grad.reshape(channels, group_count, group_size, width).transpose(1, 2, 0, 3)
    slot_numbers = jnp.arange(visible, dtype=jnp.int32)

    def backward(totals, inputs):
        taps_part, weights_part, slots_part, gradient_portion = inputs
        texture_lookup = sample_matrix(taps_part, weights_part, texel).reshape(
            group_size, width, texel
        )
        texel_gradient = jnp.einsum(
            "rzs,rsu->rzu", gradient_portion, texture_lookup, preferred_element_type=jnp.float32
        )
        selector = (slots_part[:, None] == slot_numbers[None, :]).astype(jnp.float32)
        added = jnp.einsum("gv,gct->vct", selector, texel_gradient, precision=lax.Precision.HIGHEST)
        return (totals + added, None)

    start = jnp.zeros((visible, channels, texel), jnp.float32)
    slot_grad, unused = lax.scan(
        backward, start, (taps_grouped, weights_grouped, slots_grouped, grad_grouped)
    )
    return (rendered, slot_grad.reshape(visible, channels * texel), weight_local)


def per_device(texture, requests, block_slot, texel_cell, uv_frac, conv_weight, cotangent):
    owners = lax.axis_size("tex")
    frame_count = lax.axis_size("frames")
    tile_count = texture.shape[0]
    tile_width = texture.shape[1]
    wanted_ids = requests.reshape(owners, -1)
    wanted = lax.all_to_all(wanted_ids, "tex", split_axis=0, concat_axis=0, tiled=True)
    served = jnp.take(texture, wanted.reshape(-1), axis=0).reshape(
        wanted.shape[0], wanted.shape[1], tile_width
    )
    returned_tiles = lax.all_to_all(served, "tex", split_axis=0, concat_axis=0, tiled=True)
    fetched = returned_tiles
    per_owner = fetched.shape[1]
    visible = owners * per_owner
    fetched = fetched.reshape(visible, CH, tile_width // CH)
    rendered, slot_grad, weight_local = render_one(
        fetched, block_slot[0], texel_cell[0], uv_frac[0], conv_weight, cotangent[0]
    )
    columns = tile_width // frame_count
    weight_size = weight_local.size
    chunk = -(-weight_size // frame_count)
    request_count = requests.shape[1]
    extra = -(-(chunk + request_count) // columns)
    weight_rows = jnp.pad(weight_local.reshape(-1), (0, chunk * frame_count - weight_size))
    side_row = jnp.concatenate(
        [
            weight_rows.reshape(frame_count, chunk),
            jnp.broadcast_to(requests.astype(jnp.float32), (frame_count, request_count)),
            jnp.zeros((frame_count, extra * columns - chunk - request_count), jnp.float32),
        ],
        axis=1,
    ).reshape(frame_count, extra, columns)
    spread = slot_grad.reshape(visible, frame_count, columns).transpose(1, 0, 2)
    spread = jnp.concatenate([spread, side_row], axis=1)
    gathered = lax.all_to_all(spread, "frames", split_axis=0, concat_axis=0, tiled=True)
    side = gathered[:, visible:].reshape(frame_count, extra * columns)
    frame_weight = jnp.sum(side[:, :chunk], axis=0)
    senders = side[:, chunk : chunk + request_count].astype(jnp.int32)
    senders = senders.reshape(frame_count, owners, per_owner)
    gathered = gathered[:, :visible].reshape(frame_count, owners, per_owner, columns)
    tile_numbers = jnp.arange(tile_count, dtype=jnp.int32)
    selector = (senders[None] == tile_numbers[:, None, None, None]).astype(jnp.float32)
    partial = jnp.einsum(
        "qfoj,fojc->oqc", selector, gathered, precision=lax.Precision.HIGHEST
    )
    weight_tail = -(-chunk // columns) * columns
    weight_block = jnp.pad(frame_weight, (0, weight_tail - chunk)).reshape(1, -1, columns)
    partial = jnp.concatenate(
        [partial, jnp.broadcast_to(weight_block, (owners,) + weight_block.shape[1:])], axis=1
    )
    collected = jnp.sum(lax.all_to_all(partial, "tex", 0, 0, tiled=True), axis=0)
    texture_grad = collected[:tile_count]
    chunk_total = collected[tile_count:].reshape(-1)[:chunk]
    shared = lax.all_to_all(
        jnp.broadcast_to(chunk_total[None], (frame_count, chunk)), "frames", 0, 0, tiled=True
    )
    norm_scale = 1.0 / math.sqrt(frame_count * owners * cotangent.shape[2])
    weight_grad = shared.reshape(-1)[:weight_size].reshape(weight_local.shape) * norm_scale
    return (rendered[None], texture_grad, weight_grad)


def solution(mesh):
    placed = (
        P("tex", None),
        P(("frames", "tex"), None),
        P(("frames", "tex"), None),
        P(("frames", "tex"), None),
        P(("frames", "tex"), None, None),
        P(),
        P(("frames", "tex"), None, None),
    )
    return jax.shard_map(
        per_device,
        mesh=mesh,
        in_specs=placed,
        out_specs=(P(("frames", "tex"), None, None), P("tex", "frames"), P()),
        check_vma=False,
    )
```

```python
import math

import jax
import jax.numpy as jnp
from jax import lax
from jax.sharding import PartitionSpec as P

CH = 16


def taps_and_weights(cell_row, frac_row, side):
    column = cell_row % (side - 1)
    row_index = cell_row // (side - 1)
    corner = row_index * side + column
    texel_taps = jnp.stack([corner, corner + 1, corner + side, corner + side + 1])
    frac_x = frac_row[0]
    frac_y = frac_row[1]
    weights = jnp.stack(
        [
            (1.0 - frac_x) * (1.0 - frac_y),
            frac_x * (1.0 - frac_y),
            (1.0 - frac_x) * frac_y,
            frac_x * frac_y,
        ]
    )
    return (texel_taps, weights)


def sample_matrix(texel_taps, weights, texel):
    positions = lax.broadcasted_iota(jnp.int32, (texel_taps.shape[1], texel), 1)
    matrix = jnp.zeros((texel_taps.shape[1], texel), jnp.float32)
    for number in range(4):
        matrix = matrix + jnp.where(
            texel_taps[number][:, None] == positions, weights[number][:, None], jnp.float32(0.0)
        )
    return matrix.astype(jnp.bfloat16)


def shifted(picture, shift_y, shift_x):
    height = picture.shape[1]
    width = picture.shape[2]
    padded_input = jnp.pad(picture, ((0, 0), (1, 1), (1, 1)))
    return padded_input[:, 1 + shift_y : 1 + shift_y + height, 1 + shift_x : 1 + shift_x + width]


def render_one(fetched, slot_row, cell_row, frac_row, conv_weight, cot_row):
    visible = fetched.shape[0]
    channels = fetched.shape[1]
    texel = fetched.shape[2]
    side = math.isqrt(texel)
    height = slot_row.shape[0]
    width = cell_row.shape[0] // height
    group_size = math.gcd(height, 16)
    group_count = height // group_size
    texel_taps, weights = taps_and_weights(cell_row, frac_row, side)
    taps_grouped = texel_taps.reshape(4, group_count, group_size * width).transpose(1, 0, 2)
    weights_grouped = weights.reshape(4, group_count, group_size * width).transpose(1, 0, 2)
    slots_grouped = slot_row.reshape(group_count, group_size)

    def forward(inputs):
        taps_part, weights_part, slots_part = inputs
        texture_lookup = sample_matrix(taps_part, weights_part, texel).reshape(
            group_size, width, texel
        )
        selected_entries = jnp.take(fetched, slots_part, axis=0)
        feature_maps = jnp.einsum(
            "qfm,qzm->qfz", selected_entries, texture_lookup, preferred_element_type=jnp.float32
        )
        return feature_maps.astype(jnp.bfloat16)

    grouped_features = lax.map(forward, (taps_grouped, weights_grouped, slots_grouped))
    feature_maps = grouped_features.transpose(2, 0, 1, 3).reshape(channels, height, width)
    offsets = [(shift_y, shift_x) for shift_y in (-1, 0, 1) for shift_x in (-1, 0, 1)]
    columns = jnp.concatenate(
        [shifted(feature_maps, shift_y, shift_x) for shift_y, shift_x in offsets], axis=0
    )
    columns = columns.reshape(9 * channels, height * width)
    preact = jnp.dot(conv_weight, columns, preferred_element_type=jnp.float32)
    sigmoid_pre = jax.nn.sigmoid(preact)
    rendered = (preact * sigmoid_pre).astype(jnp.bfloat16)
    pre_grad = (
        cot_row.astype(jnp.float32) * sigmoid_pre * (1.0 + preact * (1.0 - sigmoid_pre))
    ).astype(jnp.bfloat16)
    weight_local = jnp.einsum("op,kp->ok", pre_grad, columns, preferred_element_type=jnp.float32)
    col_grad = jnp.einsum("ok,op->kp", conv_weight, pre_grad, preferred_element_type=jnp.float32)
    col_grad = col_grad.reshape(9, channels, height, width)
    feat_grad = jnp.zeros((channels, height, width), jnp.float32)
    for number in range(9):
        shift_y, shift_x = offsets[number]
        feat_grad = feat_grad + shifted(col_grad[number], -shift_y, -shift_x)
    feat_grad = feat_grad.astype(jnp.bfloat16)
    grad_grouped = feat_grad.reshape(channels, group_count, group_size, width).transpose(1, 2, 0, 3)
    slot_numbers = jnp.arange(visible, dtype=jnp.int32)

    def backward(totals, inputs):
        taps_part, weights_part, slots_part, gradient_portion = inputs
        texture_lookup = sample_matrix(taps_part, weights_part, texel).reshape(
            group_size, width, texel
        )
        texel_gradient = jnp.einsum(
            "rzs,rsu->rzu", gradient_portion, texture_lookup, preferred_element_type=jnp.float32
        )
        selector = (slots_part[:, None] == slot_numbers[None, :]).astype(jnp.float32)
        added = jnp.einsum("gv,gct->vct", selector, texel_gradient, precision=lax.Precision.HIGHEST)
        return (totals + added, None)

    start = jnp.zeros((visible, channels, texel), jnp.float32)
    slot_grad, unused = lax.scan(
        backward, start, (taps_grouped, weights_grouped, slots_grouped, grad_grouped)
    )
    return (rendered, slot_grad.reshape(visible, channels * texel), weight_local)


def per_device(texture, requests, block_slot, texel_cell, uv_frac, conv_weight, cotangent):
    owners = lax.axis_size("tex")
    frame_count = lax.axis_size("frames")
    tile_count = texture.shape[0]
    tile_width = texture.shape[1]
    wanted_ids = requests.reshape(owners, -1)
    wanted = lax.all_to_all(wanted_ids, "tex", split_axis=0, concat_axis=0, tiled=True)
    served = jnp.take(texture, wanted.reshape(-1), axis=0).reshape(
        wanted.shape[0], wanted.shape[1], tile_width
    )
    returned_tiles = lax.all_to_all(served, "tex", split_axis=0, concat_axis=0, tiled=True)
    fetched = returned_tiles
    per_owner = fetched.shape[1]
    visible = owners * per_owner
    fetched = fetched.reshape(visible, CH, tile_width // CH)
    rendered, slot_grad, weight_local = render_one(
        fetched, block_slot[0], texel_cell[0], uv_frac[0], conv_weight, cotangent[0]
    )
    columns = tile_width // frame_count
    weight_size = weight_local.size
    chunk = -(-weight_size // frame_count)
    request_count = requests.shape[1]
    weight_rows = jnp.pad(weight_local.reshape(-1), (0, chunk * frame_count - weight_size))
    weight_rows = weight_rows.reshape(frame_count, chunk)
    weight_high = weight_rows.astype(jnp.bfloat16)
    weight_low = (weight_rows - weight_high.astype(jnp.float32)).astype(jnp.bfloat16)
    extra = -(-(2 * chunk + request_count) // columns)
    side_row = jnp.concatenate(
        [
            weight_high,
            weight_low,
            jnp.broadcast_to(requests.astype(jnp.bfloat16), (frame_count, request_count)),
            jnp.zeros((frame_count, extra * columns - 2 * chunk - request_count), jnp.bfloat16),
        ],
        axis=1,
    ).reshape(frame_count, extra, columns)
    spread = slot_grad.reshape(visible, frame_count, columns).transpose(1, 0, 2)
    spread = jnp.concatenate([spread.astype(jnp.bfloat16), side_row], axis=1)
    gathered = lax.all_to_all(spread, "frames", split_axis=0, concat_axis=0, tiled=True)
    side = gathered[:, visible:].reshape(frame_count, extra * columns).astype(jnp.float32)
    frame_weight = jnp.sum(side[:, :chunk] + side[:, chunk : 2 * chunk], axis=0)
    senders = side[:, 2 * chunk : 2 * chunk + request_count].astype(jnp.int32)
    senders = senders.reshape(frame_count, owners, per_owner)
    gathered = gathered[:, :visible].astype(jnp.float32)
    gathered = gathered.reshape(frame_count, owners, per_owner, columns)
    tile_numbers = jnp.arange(tile_count, dtype=jnp.int32)
    selector = (senders[None] == tile_numbers[:, None, None, None]).astype(jnp.float32)
    partial = jnp.einsum(
        "qfoj,fojc->oqc", selector, gathered, precision=lax.Precision.HIGHEST
    )
    weight_tail = -(-chunk // columns) * columns
    weight_block = jnp.pad(frame_weight, (0, weight_tail - chunk)).reshape(1, -1, columns)
    partial = jnp.concatenate(
        [partial, jnp.broadcast_to(weight_block, (owners,) + weight_block.shape[1:])], axis=1
    )
    collected = jnp.sum(lax.all_to_all(partial, "tex", 0, 0, tiled=True), axis=0)
    texture_grad = collected[:tile_count]
    chunk_total = collected[tile_count:].reshape(-1)[:chunk]
    shared = lax.all_to_all(
        jnp.broadcast_to(chunk_total[None], (frame_count, chunk)), "frames", 0, 0, tiled=True
    )
    norm_scale = 1.0 / math.sqrt(frame_count * owners * cotangent.shape[2])
    weight_grad = shared.reshape(-1)[:weight_size].reshape(weight_local.shape) * norm_scale
    return (rendered[None], texture_grad, weight_grad)


def solution(mesh):
    placed = (
        P("tex", None),
        P(("frames", "tex"), None),
        P(("frames", "tex"), None),
        P(("frames", "tex"), None),
        P(("frames", "tex"), None, None),
        P(),
        P(("frames", "tex"), None, None),
    )
    return jax.shard_map(
        per_device,
        mesh=mesh,
        in_specs=placed,
        out_specs=(P(("frames", "tex"), None, None), P("tex", "frames"), P()),
        check_vma=False,
    )
```

```python
import math

import jax
import jax.numpy as jnp
from jax import lax
from jax.sharding import PartitionSpec as P

CH = 16


def taps_and_weights(cell_row, frac_row, side):
    column = cell_row % (side - 1)
    row_index = cell_row // (side - 1)
    corner = row_index * side + column
    texel_taps = jnp.stack([corner, corner + 1, corner + side, corner + side + 1])
    frac_x = frac_row[0]
    frac_y = frac_row[1]
    weights = jnp.stack(
        [
            (1.0 - frac_x) * (1.0 - frac_y),
            frac_x * (1.0 - frac_y),
            (1.0 - frac_x) * frac_y,
            frac_x * frac_y,
        ]
    )
    return (texel_taps, weights)


def sample_matrix(texel_taps, weights, texel):
    positions = lax.broadcasted_iota(jnp.int32, (texel_taps.shape[1], texel), 1)
    matrix = jnp.zeros((texel_taps.shape[1], texel), jnp.float32)
    for number in range(4):
        matrix = matrix + jnp.where(
            texel_taps[number][:, None] == positions, weights[number][:, None], jnp.float32(0.0)
        )
    return matrix.astype(jnp.bfloat16)


def shifted(picture, shift_y, shift_x):
    height = picture.shape[1]
    width = picture.shape[2]
    padded_input = jnp.pad(picture, ((0, 0), (1, 1), (1, 1)))
    return padded_input[:, 1 + shift_y : 1 + shift_y + height, 1 + shift_x : 1 + shift_x + width]


def render_one(fetched, slot_row, cell_row, frac_row, conv_weight, cot_row):
    visible = fetched.shape[0]
    channels = fetched.shape[1]
    texel = fetched.shape[2]
    side = math.isqrt(texel)
    height = slot_row.shape[0]
    width = cell_row.shape[0] // height
    group_size = math.gcd(height, 16)
    group_count = height // group_size
    texel_taps, weights = taps_and_weights(cell_row, frac_row, side)
    taps_grouped = texel_taps.reshape(4, group_count, group_size * width).transpose(1, 0, 2)
    weights_grouped = weights.reshape(4, group_count, group_size * width).transpose(1, 0, 2)
    slots_grouped = slot_row.reshape(group_count, group_size)

    def forward(inputs):
        taps_part, weights_part, slots_part = inputs
        texture_lookup = sample_matrix(taps_part, weights_part, texel).reshape(
            group_size, width, texel
        )
        selected_entries = jnp.take(fetched, slots_part, axis=0)
        feature_maps = jnp.einsum(
            "qfm,qzm->qfz", selected_entries, texture_lookup, preferred_element_type=jnp.float32
        )
        return feature_maps.astype(jnp.bfloat16)

    grouped_features = lax.map(forward, (taps_grouped, weights_grouped, slots_grouped))
    feature_maps = grouped_features.transpose(2, 0, 1, 3).reshape(channels, height, width)
    offsets = [(shift_y, shift_x) for shift_y in (-1, 0, 1) for shift_x in (-1, 0, 1)]
    columns = jnp.concatenate(
        [shifted(feature_maps, shift_y, shift_x) for shift_y, shift_x in offsets], axis=0
    )
    columns = columns.reshape(9 * channels, height * width)
    preact = jnp.dot(conv_weight, columns, preferred_element_type=jnp.float32)
    sigmoid_pre = jax.nn.sigmoid(preact)
    rendered = (preact * sigmoid_pre).astype(jnp.bfloat16)
    pre_grad = (
        cot_row.astype(jnp.float32) * sigmoid_pre * (1.0 + preact * (1.0 - sigmoid_pre))
    ).astype(jnp.bfloat16)
    weight_local = jnp.einsum("op,kp->ok", pre_grad, columns, preferred_element_type=jnp.float32)
    col_grad = jnp.einsum("ok,op->kp", conv_weight, pre_grad, preferred_element_type=jnp.float32)
    col_grad = col_grad.reshape(9, channels, height, width)
    feat_grad = jnp.zeros((channels, height, width), jnp.float32)
    for number in range(9):
        shift_y, shift_x = offsets[number]
        feat_grad = feat_grad + shifted(col_grad[number], -shift_y, -shift_x)
    feat_grad = feat_grad.astype(jnp.bfloat16)
    grad_grouped = feat_grad.reshape(channels, group_count, group_size, width).transpose(1, 2, 0, 3)
    slot_numbers = jnp.arange(visible, dtype=jnp.int32)

    def backward(totals, inputs):
        taps_part, weights_part, slots_part, gradient_portion = inputs
        texture_lookup = sample_matrix(taps_part, weights_part, texel).reshape(
            group_size, width, texel
        )
        texel_gradient = jnp.einsum(
            "rzs,rsu->rzu", gradient_portion, texture_lookup, preferred_element_type=jnp.float32
        )
        selector = (slots_part[:, None] == slot_numbers[None, :]).astype(jnp.float32)
        added = jnp.einsum("gv,gct->vct", selector, texel_gradient, precision=lax.Precision.HIGHEST)
        return (totals + added, None)

    start = jnp.zeros((visible, channels, texel), jnp.float32)
    slot_grad, unused = lax.scan(
        backward, start, (taps_grouped, weights_grouped, slots_grouped, grad_grouped)
    )
    return (rendered, slot_grad.reshape(visible, channels * texel), weight_local)


def render_flat(fetched, slot_row, lookup, conv_weight, cot_row):
    visible = fetched.shape[0]
    channels = fetched.shape[1]
    texel = fetched.shape[2]
    height = slot_row.shape[0]
    width = lookup.shape[1]
    selected_entries = jnp.take(fetched, slot_row, axis=0)
    feature_maps = jnp.einsum(
        "qfm,qzm->fqz", selected_entries, lookup, preferred_element_type=jnp.float32
    ).astype(jnp.bfloat16)
    offsets = [(shift_y, shift_x) for shift_y in (-1, 0, 1) for shift_x in (-1, 0, 1)]
    columns = jnp.concatenate(
        [shifted(feature_maps, shift_y, shift_x) for shift_y, shift_x in offsets], axis=0
    )
    columns = columns.reshape(9 * channels, height * width)
    preact = jnp.dot(conv_weight, columns, preferred_element_type=jnp.float32)
    sigmoid_pre = jax.nn.sigmoid(preact)
    rendered = (preact * sigmoid_pre).astype(jnp.bfloat16)
    pre_grad = (
        cot_row.astype(jnp.float32) * sigmoid_pre * (1.0 + preact * (1.0 - sigmoid_pre))
    ).astype(jnp.bfloat16)
    weight_local = jnp.einsum("op,kp->ok", pre_grad, columns, preferred_element_type=jnp.float32)
    col_grad = jnp.einsum("ok,op->kp", conv_weight, pre_grad, preferred_element_type=jnp.float32)
    col_grad = col_grad.reshape(9, channels, height, width)
    feat_grad = jnp.zeros((channels, height, width), jnp.float32)
    for number in range(9):
        shift_y, shift_x = offsets[number]
        feat_grad = feat_grad + shifted(col_grad[number], -shift_y, -shift_x)
    feat_grad = feat_grad.astype(jnp.bfloat16)
    texel_gradient = jnp.einsum(
        "zrs,rsu->rzu", feat_grad, lookup, preferred_element_type=jnp.float32
    )
    slot_numbers = jnp.arange(visible, dtype=jnp.int32)
    selector = (slot_row[:, None] == slot_numbers[None, :]).astype(jnp.float32)
    slot_grad = jnp.einsum(
        "gv,gct->vct", selector, texel_gradient, precision=lax.Precision.HIGHEST
    )
    return (rendered, slot_grad.reshape(visible, channels * texel), weight_local)


def per_device(texture, requests, block_slot, texel_cell, uv_frac, conv_weight, cotangent):
    owners = lax.axis_size("tex")
    frame_count = lax.axis_size("frames")
    tile_count = texture.shape[0]
    tile_width = texture.shape[1]
    texel = tile_width // CH
    height = block_slot.shape[1]
    texel_taps, weights = taps_and_weights(texel_cell[0], uv_frac[0], math.isqrt(texel))
    lookup = sample_matrix(texel_taps, weights, texel).reshape(height, -1, texel)
    lookup = lax.optimization_barrier(lookup)
    wanted_ids = requests.reshape(owners, -1)
    wanted = lax.all_to_all(wanted_ids, "tex", split_axis=0, concat_axis=0, tiled=True)
    served = jnp.take(texture, wanted.reshape(-1), axis=0).reshape(
        wanted.shape[0], wanted.shape[1], tile_width
    )
    returned_tiles = lax.all_to_all(served, "tex", split_axis=0, concat_axis=0, tiled=True)
    fetched = returned_tiles
    per_owner = fetched.shape[1]
    visible = owners * per_owner
    fetched = fetched.reshape(visible, CH, tile_width // CH)
    rendered, slot_grad, weight_local = render_flat(
        fetched, block_slot[0], lookup, conv_weight, cotangent[0]
    )
    columns = tile_width // frame_count
    weight_size = weight_local.size
    chunk = -(-weight_size // frame_count)
    request_count = requests.shape[1]
    weight_rows = jnp.pad(weight_local.reshape(-1), (0, chunk * frame_count - weight_size))
    weight_rows = weight_rows.reshape(frame_count, chunk)
    weight_high = weight_rows.astype(jnp.bfloat16)
    weight_low = (weight_rows - weight_high.astype(jnp.float32)).astype(jnp.bfloat16)
    extra = -(-(2 * chunk + request_count) // columns)
    side_row = jnp.concatenate(
        [
            weight_high,
            weight_low,
            jnp.broadcast_to(requests.astype(jnp.bfloat16), (frame_count, request_count)),
            jnp.zeros((frame_count, extra * columns - 2 * chunk - request_count), jnp.bfloat16),
        ],
        axis=1,
    ).reshape(frame_count, extra, columns)
    spread = slot_grad.reshape(visible, frame_count, columns).transpose(1, 0, 2)
    spread = jnp.concatenate([spread.astype(jnp.bfloat16), side_row], axis=1)
    gathered = lax.all_to_all(spread, "frames", split_axis=0, concat_axis=0, tiled=True)
    side = gathered[:, visible:].reshape(frame_count, extra * columns).astype(jnp.float32)
    frame_weight = jnp.sum(side[:, :chunk] + side[:, chunk : 2 * chunk], axis=0)
    senders = side[:, 2 * chunk : 2 * chunk + request_count].astype(jnp.int32)
    senders = senders.reshape(frame_count, owners, per_owner)
    gathered = gathered[:, :visible].astype(jnp.float32)
    gathered = gathered.reshape(frame_count, owners, per_owner, columns)
    tile_numbers = jnp.arange(tile_count, dtype=jnp.int32)
    selector = (senders[None] == tile_numbers[:, None, None, None]).astype(jnp.float32)
    partial = jnp.einsum(
        "qfoj,fojc->oqc", selector, gathered, precision=lax.Precision.HIGHEST
    )
    weight_tail = -(-chunk // columns) * columns
    weight_block = jnp.pad(frame_weight, (0, weight_tail - chunk)).reshape(1, -1, columns)
    partial = jnp.concatenate(
        [partial, jnp.broadcast_to(weight_block, (owners,) + weight_block.shape[1:])], axis=1
    )
    collected = jnp.sum(lax.all_to_all(partial, "tex", 0, 0, tiled=True), axis=0)
    texture_grad = collected[:tile_count]
    chunk_total = collected[tile_count:].reshape(-1)[:chunk]
    shared = lax.all_to_all(
        jnp.broadcast_to(chunk_total[None], (frame_count, chunk)), "frames", 0, 0, tiled=True
    )
    norm_scale = 1.0 / math.sqrt(frame_count * owners * cotangent.shape[2])
    weight_grad = shared.reshape(-1)[:weight_size].reshape(weight_local.shape) * norm_scale
    return (rendered[None], texture_grad, weight_grad)


def solution(mesh):
    placed = (
        P("tex", None),
        P(("frames", "tex"), None),
        P(("frames", "tex"), None),
        P(("frames", "tex"), None),
        P(("frames", "tex"), None, None),
        P(),
        P(("frames", "tex"), None, None),
    )
    return jax.shard_map(
        per_device,
        mesh=mesh,
        in_specs=placed,
        out_specs=(P(("frames", "tex"), None, None), P("tex", "frames"), P()),
        check_vma=False,
    )
```

```python
import math

import jax
import jax.numpy as jnp
from jax import lax
from jax.sharding import PartitionSpec as P

CH = 16


def taps_and_weights(cell_row, frac_row, side):
    column = cell_row % (side - 1)
    row_index = cell_row // (side - 1)
    corner = row_index * side + column
    texel_taps = jnp.stack([corner, corner + 1, corner + side, corner + side + 1])
    frac_x = frac_row[0]
    frac_y = frac_row[1]
    weights = jnp.stack(
        [
            (1.0 - frac_x) * (1.0 - frac_y),
            frac_x * (1.0 - frac_y),
            (1.0 - frac_x) * frac_y,
            frac_x * frac_y,
        ]
    )
    return (texel_taps, weights)


def sample_matrix(texel_taps, weights, texel):
    positions = lax.broadcasted_iota(jnp.int32, (texel_taps.shape[1], texel), 1)
    matrix = jnp.zeros((texel_taps.shape[1], texel), jnp.float32)
    for number in range(4):
        matrix = matrix + jnp.where(
            texel_taps[number][:, None] == positions, weights[number][:, None], jnp.float32(0.0)
        )
    return matrix.astype(jnp.bfloat16)


def shifted(picture, shift_y, shift_x):
    height = picture.shape[1]
    width = picture.shape[2]
    padded_input = jnp.pad(picture, ((0, 0), (1, 1), (1, 1)))
    return padded_input[:, 1 + shift_y : 1 + shift_y + height, 1 + shift_x : 1 + shift_x + width]


def render_one(fetched, slot_row, cell_row, frac_row, conv_weight, cot_row):
    visible = fetched.shape[0]
    channels = fetched.shape[1]
    texel = fetched.shape[2]
    side = math.isqrt(texel)
    height = slot_row.shape[0]
    width = cell_row.shape[0] // height
    group_size = math.gcd(height, 16)
    group_count = height // group_size
    texel_taps, weights = taps_and_weights(cell_row, frac_row, side)
    taps_grouped = texel_taps.reshape(4, group_count, group_size * width).transpose(1, 0, 2)
    weights_grouped = weights.reshape(4, group_count, group_size * width).transpose(1, 0, 2)
    slots_grouped = slot_row.reshape(group_count, group_size)

    def forward(inputs):
        taps_part, weights_part, slots_part = inputs
        texture_lookup = sample_matrix(taps_part, weights_part, texel).reshape(
            group_size, width, texel
        )
        selected_entries = jnp.take(fetched, slots_part, axis=0)
        feature_maps = jnp.einsum(
            "qfm,qzm->qfz", selected_entries, texture_lookup, preferred_element_type=jnp.float32
        )
        return feature_maps.astype(jnp.bfloat16)

    grouped_features = lax.map(forward, (taps_grouped, weights_grouped, slots_grouped))
    feature_maps = grouped_features.transpose(2, 0, 1, 3).reshape(channels, height, width)
    offsets = [(shift_y, shift_x) for shift_y in (-1, 0, 1) for shift_x in (-1, 0, 1)]
    columns = jnp.concatenate(
        [shifted(feature_maps, shift_y, shift_x) for shift_y, shift_x in offsets], axis=0
    )
    columns = columns.reshape(9 * channels, height * width)
    preact = jnp.dot(conv_weight, columns, preferred_element_type=jnp.float32)
    sigmoid_pre = jax.nn.sigmoid(preact)
    rendered = (preact * sigmoid_pre).astype(jnp.bfloat16)
    pre_grad = (
        cot_row.astype(jnp.float32) * sigmoid_pre * (1.0 + preact * (1.0 - sigmoid_pre))
    ).astype(jnp.bfloat16)
    weight_local = jnp.einsum("op,kp->ok", pre_grad, columns, preferred_element_type=jnp.float32)
    col_grad = jnp.einsum("ok,op->kp", conv_weight, pre_grad, preferred_element_type=jnp.float32)
    col_grad = col_grad.reshape(9, channels, height, width)
    feat_grad = jnp.zeros((channels, height, width), jnp.float32)
    for number in range(9):
        shift_y, shift_x = offsets[number]
        feat_grad = feat_grad + shifted(col_grad[number], -shift_y, -shift_x)
    feat_grad = feat_grad.astype(jnp.bfloat16)
    grad_grouped = feat_grad.reshape(channels, group_count, group_size, width).transpose(1, 2, 0, 3)
    slot_numbers = jnp.arange(visible, dtype=jnp.int32)

    def backward(totals, inputs):
        taps_part, weights_part, slots_part, gradient_portion = inputs
        texture_lookup = sample_matrix(taps_part, weights_part, texel).reshape(
            group_size, width, texel
        )
        texel_gradient = jnp.einsum(
            "rzs,rsu->rzu", gradient_portion, texture_lookup, preferred_element_type=jnp.float32
        )
        selector = (slots_part[:, None] == slot_numbers[None, :]).astype(jnp.float32)
        added = jnp.einsum("gv,gct->vct", selector, texel_gradient, precision=lax.Precision.HIGHEST)
        return (totals + added, None)

    start = jnp.zeros((visible, channels, texel), jnp.float32)
    slot_grad, unused = lax.scan(
        backward, start, (taps_grouped, weights_grouped, slots_grouped, grad_grouped)
    )
    return (rendered, slot_grad.reshape(visible, channels * texel), weight_local)


def render_flat(fetched, slot_row, lookup, conv_weight, cot_row):
    visible = fetched.shape[0]
    channels = fetched.shape[1]
    texel = fetched.shape[2]
    height = slot_row.shape[0]
    width = lookup.shape[1]
    selected_entries = jnp.take(fetched, slot_row, axis=0)
    feature_maps = jnp.einsum(
        "qfm,qzm->fqz", selected_entries, lookup, preferred_element_type=jnp.float32
    ).astype(jnp.bfloat16)
    offsets = [(shift_y, shift_x) for shift_y in (-1, 0, 1) for shift_x in (-1, 0, 1)]
    columns = jnp.concatenate(
        [shifted(feature_maps, shift_y, shift_x) for shift_y, shift_x in offsets], axis=0
    )
    columns = columns.reshape(9 * channels, height * width)
    preact = jnp.dot(conv_weight, columns, preferred_element_type=jnp.float32)
    sigmoid_pre = jax.nn.sigmoid(preact)
    rendered = (preact * sigmoid_pre).astype(jnp.bfloat16)
    pre_grad = (
        cot_row.astype(jnp.float32) * sigmoid_pre * (1.0 + preact * (1.0 - sigmoid_pre))
    ).astype(jnp.bfloat16)
    weight_local = jnp.einsum("op,kp->ok", pre_grad, columns, preferred_element_type=jnp.float32)
    col_grad = jnp.einsum("ok,op->kp", conv_weight, pre_grad, preferred_element_type=jnp.float32)
    col_grad = col_grad.reshape(9, channels, height, width)
    feat_grad = jnp.zeros((channels, height, width), jnp.float32)
    for number in range(9):
        shift_y, shift_x = offsets[number]
        feat_grad = feat_grad + shifted(col_grad[number], -shift_y, -shift_x)
    feat_grad = feat_grad.astype(jnp.bfloat16)
    texel_gradient = jnp.einsum(
        "zrs,rsu->rzu", feat_grad, lookup, preferred_element_type=jnp.float32
    )
    slot_numbers = jnp.arange(visible, dtype=jnp.int32)
    selector = (slot_row[:, None] == slot_numbers[None, :]).astype(jnp.float32)
    slot_grad = jnp.einsum(
        "gv,gct->vct", selector, texel_gradient, precision=lax.Precision.HIGHEST
    )
    return (rendered, slot_grad.reshape(visible, channels * texel), weight_local)


def per_device(texture, requests, block_slot, texel_cell, uv_frac, conv_weight, cotangent):
    owners = lax.axis_size("tex")
    frame_count = lax.axis_size("frames")
    tile_count = texture.shape[0]
    tile_width = texture.shape[1]
    texel = tile_width // CH
    height = block_slot.shape[1]
    texel_taps, weights = taps_and_weights(texel_cell[0], uv_frac[0], math.isqrt(texel))
    lookup = sample_matrix(texel_taps, weights, texel).reshape(height, -1, texel)
    lookup = lax.optimization_barrier(lookup)
    wanted_ids = requests.reshape(owners, -1)
    wanted = lax.all_to_all(wanted_ids, "tex", split_axis=0, concat_axis=0, tiled=True)
    served = jnp.take(texture, wanted.reshape(-1), axis=0).reshape(
        wanted.shape[0], wanted.shape[1], tile_width
    )
    returned_tiles = lax.all_to_all(served, "tex", split_axis=0, concat_axis=0, tiled=True)
    fetched = returned_tiles
    per_owner = fetched.shape[1]
    visible = owners * per_owner
    fetched = fetched.reshape(visible, CH, tile_width // CH)
    rendered, slot_grad, weight_local = render_flat(
        fetched, block_slot[0], lookup, conv_weight, cotangent[0]
    )
    columns = tile_width // frame_count
    weight_size = weight_local.size
    chunk = -(-weight_size // frame_count)
    request_count = requests.shape[1]
    weight_rows = jnp.pad(weight_local.reshape(-1), (0, chunk * frame_count - weight_size))
    weight_rows = weight_rows.reshape(frame_count, chunk)
    weight_high = weight_rows.astype(jnp.bfloat16)
    weight_low = (weight_rows - weight_high.astype(jnp.float32)).astype(jnp.bfloat16)
    extra = -(-(2 * chunk + request_count) // columns)
    side_row = jnp.concatenate(
        [
            weight_high,
            weight_low,
            jnp.broadcast_to(requests.astype(jnp.bfloat16), (frame_count, request_count)),
            jnp.zeros((frame_count, extra * columns - 2 * chunk - request_count), jnp.bfloat16),
        ],
        axis=1,
    ).reshape(frame_count, extra, columns)
    spread = slot_grad.reshape(visible, frame_count, columns).transpose(1, 0, 2)
    spread = jnp.concatenate([spread.astype(jnp.bfloat16), side_row], axis=1)
    gathered = lax.all_to_all(spread, "frames", split_axis=0, concat_axis=0, tiled=True)
    side = gathered[:, visible:].reshape(frame_count, extra * columns).astype(jnp.float32)
    frame_weight = jnp.sum(side[:, :chunk] + side[:, chunk : 2 * chunk], axis=0)
    senders = side[:, 2 * chunk : 2 * chunk + request_count].astype(jnp.int32)
    senders = senders.reshape(frame_count, owners, per_owner)
    gathered = gathered[:, :visible].astype(jnp.float32)
    gathered = gathered.reshape(frame_count, owners, per_owner, columns)
    tile_numbers = jnp.arange(tile_count, dtype=jnp.int32)
    selector = (senders[None] == tile_numbers[:, None, None, None]).astype(jnp.float32)
    partial = jnp.einsum(
        "qfoj,fojc->oqc", selector, gathered, precision=lax.Precision.HIGHEST
    )
    weight_high = frame_weight.astype(jnp.bfloat16)
    weight_low = (frame_weight - weight_high.astype(jnp.float32)).astype(jnp.bfloat16)
    weight_tail = -(-(2 * chunk) // columns) * columns
    weight_block = jnp.pad(
        jnp.concatenate([weight_high, weight_low]), (0, weight_tail - 2 * chunk)
    ).reshape(1, -1, columns)
    partial = jnp.concatenate(
        [
            partial.astype(jnp.bfloat16),
            jnp.broadcast_to(weight_block, (owners,) + weight_block.shape[1:]),
        ],
        axis=1,
    )
    received = lax.all_to_all(partial, "tex", 0, 0, tiled=True).astype(jnp.float32)
    collected = jnp.sum(received, axis=0)
    texture_grad = collected[:tile_count]
    weight_pair = collected[tile_count:].reshape(-1)
    chunk_total = weight_pair[:chunk] + weight_pair[chunk : 2 * chunk]
    shared = lax.all_to_all(
        jnp.broadcast_to(chunk_total[None], (frame_count, chunk)), "frames", 0, 0, tiled=True
    )
    norm_scale = 1.0 / math.sqrt(frame_count * owners * cotangent.shape[2])
    weight_grad = shared.reshape(-1)[:weight_size].reshape(weight_local.shape) * norm_scale
    return (rendered[None], texture_grad, weight_grad)


def solution(mesh):
    placed = (
        P("tex", None),
        P(("frames", "tex"), None),
        P(("frames", "tex"), None),
        P(("frames", "tex"), None),
        P(("frames", "tex"), None, None),
        P(),
        P(("frames", "tex"), None, None),
    )
    return jax.shard_map(
        per_device,
        mesh=mesh,
        in_specs=placed,
        out_specs=(P(("frames", "tex"), None, None), P("tex", "frames"), P()),
        check_vma=False,
    )
```

```python
import math

import jax
import jax.numpy as jnp
from jax import lax
from jax.sharding import PartitionSpec as P

CH = 16


def taps_and_weights(cell_row, frac_row, side):
    column = cell_row % (side - 1)
    row_index = cell_row // (side - 1)
    corner = row_index * side + column
    texel_taps = jnp.stack([corner, corner + 1, corner + side, corner + side + 1])
    frac_x = frac_row[0]
    frac_y = frac_row[1]
    weights = jnp.stack(
        [
            (1.0 - frac_x) * (1.0 - frac_y),
            frac_x * (1.0 - frac_y),
            (1.0 - frac_x) * frac_y,
            frac_x * frac_y,
        ]
    )
    return (texel_taps, weights)


def sample_matrix(texel_taps, weights, texel):
    positions = lax.broadcasted_iota(jnp.int32, (texel_taps.shape[1], texel), 1)
    matrix = jnp.zeros((texel_taps.shape[1], texel), jnp.float32)
    for number in range(4):
        matrix = matrix + jnp.where(
            texel_taps[number][:, None] == positions, weights[number][:, None], jnp.float32(0.0)
        )
    return matrix.astype(jnp.bfloat16)


def shifted(picture, shift_y, shift_x):
    height = picture.shape[1]
    width = picture.shape[2]
    padded_input = jnp.pad(picture, ((0, 0), (1, 1), (1, 1)))
    return padded_input[:, 1 + shift_y : 1 + shift_y + height, 1 + shift_x : 1 + shift_x + width]


def render_one(fetched, slot_row, cell_row, frac_row, conv_weight, cot_row):
    visible = fetched.shape[0]
    channels = fetched.shape[1]
    texel = fetched.shape[2]
    side = math.isqrt(texel)
    height = slot_row.shape[0]
    width = cell_row.shape[0] // height
    group_size = math.gcd(height, 16)
    group_count = height // group_size
    texel_taps, weights = taps_and_weights(cell_row, frac_row, side)
    taps_grouped = texel_taps.reshape(4, group_count, group_size * width).transpose(1, 0, 2)
    weights_grouped = weights.reshape(4, group_count, group_size * width).transpose(1, 0, 2)
    slots_grouped = slot_row.reshape(group_count, group_size)

    def forward(inputs):
        taps_part, weights_part, slots_part = inputs
        texture_lookup = sample_matrix(taps_part, weights_part, texel).reshape(
            group_size, width, texel
        )
        selected_entries = jnp.take(fetched, slots_part, axis=0)
        feature_maps = jnp.einsum(
            "qfm,qzm->qfz", selected_entries, texture_lookup, preferred_element_type=jnp.float32
        )
        return feature_maps.astype(jnp.bfloat16)

    grouped_features = lax.map(forward, (taps_grouped, weights_grouped, slots_grouped))
    feature_maps = grouped_features.transpose(2, 0, 1, 3).reshape(channels, height, width)
    offsets = [(shift_y, shift_x) for shift_y in (-1, 0, 1) for shift_x in (-1, 0, 1)]
    columns = jnp.concatenate(
        [shifted(feature_maps, shift_y, shift_x) for shift_y, shift_x in offsets], axis=0
    )
    columns = columns.reshape(9 * channels, height * width)
    preact = jnp.dot(conv_weight, columns, preferred_element_type=jnp.float32)
    sigmoid_pre = jax.nn.sigmoid(preact)
    rendered = (preact * sigmoid_pre).astype(jnp.bfloat16)
    pre_grad = (
        cot_row.astype(jnp.float32) * sigmoid_pre * (1.0 + preact * (1.0 - sigmoid_pre))
    ).astype(jnp.bfloat16)
    weight_local = jnp.einsum("op,kp->ok", pre_grad, columns, preferred_element_type=jnp.float32)
    col_grad = jnp.einsum("ok,op->kp", conv_weight, pre_grad, preferred_element_type=jnp.float32)
    col_grad = col_grad.reshape(9, channels, height, width)
    feat_grad = jnp.zeros((channels, height, width), jnp.float32)
    for number in range(9):
        shift_y, shift_x = offsets[number]
        feat_grad = feat_grad + shifted(col_grad[number], -shift_y, -shift_x)
    feat_grad = feat_grad.astype(jnp.bfloat16)
    grad_grouped = feat_grad.reshape(channels, group_count, group_size, width).transpose(1, 2, 0, 3)
    slot_numbers = jnp.arange(visible, dtype=jnp.int32)

    def backward(totals, inputs):
        taps_part, weights_part, slots_part, gradient_portion = inputs
        texture_lookup = sample_matrix(taps_part, weights_part, texel).reshape(
            group_size, width, texel
        )
        texel_gradient = jnp.einsum(
            "rzs,rsu->rzu", gradient_portion, texture_lookup, preferred_element_type=jnp.float32
        )
        selector = (slots_part[:, None] == slot_numbers[None, :]).astype(jnp.float32)
        added = jnp.einsum("gv,gct->vct", selector, texel_gradient, precision=lax.Precision.HIGHEST)
        return (totals + added, None)

    start = jnp.zeros((visible, channels, texel), jnp.float32)
    slot_grad, unused = lax.scan(
        backward, start, (taps_grouped, weights_grouped, slots_grouped, grad_grouped)
    )
    return (rendered, slot_grad.reshape(visible, channels * texel), weight_local)


def render_flat(fetched, slot_row, lookup, conv_weight, cot_row):
    visible = fetched.shape[0]
    channels = fetched.shape[1]
    texel = fetched.shape[2]
    height = slot_row.shape[0]
    width = lookup.shape[1]
    selected_entries = jnp.take(fetched, slot_row, axis=0, mode="clip")
    feature_maps = jnp.einsum(
        "qfm,qzm->fqz", selected_entries, lookup, preferred_element_type=jnp.float32
    ).astype(jnp.bfloat16)
    offsets = [(shift_y, shift_x) for shift_y in (-1, 0, 1) for shift_x in (-1, 0, 1)]
    columns = jnp.concatenate(
        [shifted(feature_maps, shift_y, shift_x) for shift_y, shift_x in offsets], axis=0
    )
    columns = columns.reshape(9 * channels, height * width)
    preact = jnp.dot(conv_weight, columns, preferred_element_type=jnp.float32)
    sigmoid_pre = jax.nn.sigmoid(preact)
    rendered = (preact * sigmoid_pre).astype(jnp.bfloat16)
    pre_grad = (
        cot_row.astype(jnp.float32) * sigmoid_pre * (1.0 + preact * (1.0 - sigmoid_pre))
    ).astype(jnp.bfloat16)
    weight_local = jnp.einsum("op,kp->ok", pre_grad, columns, preferred_element_type=jnp.float32)
    col_grad = jnp.einsum("ok,op->kp", conv_weight, pre_grad, preferred_element_type=jnp.float32)
    col_grad = col_grad.reshape(9, channels, height, width)
    feat_grad = jnp.zeros((channels, height, width), jnp.float32)
    for number in range(9):
        shift_y, shift_x = offsets[number]
        feat_grad = feat_grad + shifted(col_grad[number], -shift_y, -shift_x)
    feat_grad = feat_grad.astype(jnp.bfloat16)
    texel_gradient = jnp.einsum(
        "zrs,rsu->rzu", feat_grad, lookup, preferred_element_type=jnp.float32
    )
    slot_numbers = jnp.arange(visible, dtype=jnp.int32)
    selector = (slot_row[:, None] == slot_numbers[None, :]).astype(jnp.float32)
    slot_grad = jnp.einsum(
        "gv,gct->vct", selector, texel_gradient, precision=lax.Precision.HIGHEST
    )
    return (rendered, slot_grad.reshape(visible, channels * texel), weight_local)


def per_device(texture, requests, block_slot, texel_cell, uv_frac, conv_weight, cotangent):
    owners = lax.axis_size("tex")
    frame_count = lax.axis_size("frames")
    tile_count = texture.shape[0]
    tile_width = texture.shape[1]
    texel = tile_width // CH
    height = block_slot.shape[1]
    texel_taps, weights = taps_and_weights(texel_cell[0], uv_frac[0], math.isqrt(texel))
    lookup = sample_matrix(texel_taps, weights, texel).reshape(height, -1, texel)
    lookup = lax.optimization_barrier(lookup)
    wanted_ids = requests.reshape(owners, -1)
    wanted = lax.all_to_all(wanted_ids, "tex", split_axis=0, concat_axis=0, tiled=True)
    per_owner = wanted.shape[1]
    visible = owners * per_owner
    served = jnp.take(
        texture.reshape(tile_count, CH, texel), wanted.reshape(-1), axis=0, mode="clip"
    ).reshape(owners, per_owner * CH, texel)
    fetched = lax.all_to_all(served, "tex", split_axis=0, concat_axis=0, tiled=True)
    fetched = fetched.reshape(visible, CH, texel)
    rendered, slot_grad, weight_local = render_flat(
        fetched, block_slot[0], lookup, conv_weight, cotangent[0]
    )
    columns = tile_width // frame_count
    weight_size = weight_local.size
    chunk = -(-weight_size // frame_count)
    request_count = requests.shape[1]
    weight_rows = jnp.pad(weight_local.reshape(-1), (0, chunk * frame_count - weight_size))
    weight_rows = weight_rows.reshape(frame_count, chunk)
    weight_high = weight_rows.astype(jnp.bfloat16)
    weight_low = (weight_rows - weight_high.astype(jnp.float32)).astype(jnp.bfloat16)
    extra = -(-(2 * chunk + request_count) // columns)
    side_row = jnp.concatenate(
        [
            weight_high,
            weight_low,
            jnp.broadcast_to(requests.astype(jnp.bfloat16), (frame_count, request_count)),
            jnp.zeros((frame_count, extra * columns - 2 * chunk - request_count), jnp.bfloat16),
        ],
        axis=1,
    ).reshape(frame_count, extra, columns)
    spread = slot_grad.reshape(visible, frame_count, columns).transpose(1, 0, 2)
    spread = jnp.concatenate([spread.astype(jnp.bfloat16), side_row], axis=1)
    gathered = lax.all_to_all(spread, "frames", split_axis=0, concat_axis=0, tiled=True)
    side = gathered[:, visible:].reshape(frame_count, extra * columns).astype(jnp.float32)
    frame_weight = jnp.sum(side[:, :chunk] + side[:, chunk : 2 * chunk], axis=0)
    senders = side[:, 2 * chunk : 2 * chunk + request_count].astype(jnp.int32)
    senders = senders.reshape(frame_count, owners, per_owner)
    gathered = gathered[:, :visible].astype(jnp.float32)
    gathered = gathered.reshape(frame_count, owners, per_owner, columns)
    tile_numbers = jnp.arange(tile_count, dtype=jnp.int32)
    selector = (senders[None] == tile_numbers[:, None, None, None]).astype(jnp.float32)
    partial = jnp.einsum(
        "qfoj,fojc->oqc", selector, gathered, precision=lax.Precision.HIGHEST
    )
    weight_high = frame_weight.astype(jnp.bfloat16)
    weight_low = (frame_weight - weight_high.astype(jnp.float32)).astype(jnp.bfloat16)
    weight_tail = -(-(2 * chunk) // columns) * columns
    weight_block = jnp.pad(
        jnp.concatenate([weight_high, weight_low]), (0, weight_tail - 2 * chunk)
    ).reshape(1, -1, columns)
    partial = jnp.concatenate(
        [
            partial.astype(jnp.bfloat16),
            jnp.broadcast_to(weight_block, (owners,) + weight_block.shape[1:]),
        ],
        axis=1,
    )
    received = lax.all_to_all(partial, "tex", 0, 0, tiled=True).astype(jnp.float32)
    collected = jnp.sum(received, axis=0)
    texture_grad = collected[:tile_count]
    weight_pair = collected[tile_count:].reshape(-1)
    chunk_total = weight_pair[:chunk] + weight_pair[chunk : 2 * chunk]
    shared = lax.all_to_all(
        jnp.broadcast_to(chunk_total[None], (frame_count, chunk)), "frames", 0, 0, tiled=True
    )
    norm_scale = 1.0 / math.sqrt(frame_count * owners * cotangent.shape[2])
    weight_grad = shared.reshape(-1)[:weight_size].reshape(weight_local.shape) * norm_scale
    return (rendered[None], texture_grad, weight_grad)


def solution(mesh):
    placed = (
        P("tex", None),
        P(("frames", "tex"), None),
        P(("frames", "tex"), None),
        P(("frames", "tex"), None),
        P(("frames", "tex"), None, None),
        P(),
        P(("frames", "tex"), None, None),
    )
    return jax.shard_map(
        per_device,
        mesh=mesh,
        in_specs=placed,
        out_specs=(P(("frames", "tex"), None, None), P("tex", "frames"), P()),
        check_vma=False,
    )
```

```python
import math

import jax
import jax.numpy as jnp
from jax import lax
from jax.sharding import PartitionSpec as P

CH = 16


def taps_and_weights(cell_row, frac_row, side):
    column = cell_row % (side - 1)
    row_index = cell_row // (side - 1)
    corner = row_index * side + column
    texel_taps = jnp.stack([corner, corner + 1, corner + side, corner + side + 1])
    frac_x = frac_row[0]
    frac_y = frac_row[1]
    weights = jnp.stack(
        [
            (1.0 - frac_x) * (1.0 - frac_y),
            frac_x * (1.0 - frac_y),
            (1.0 - frac_x) * frac_y,
            frac_x * frac_y,
        ]
    )
    return (texel_taps, weights)


def sample_matrix(texel_taps, weights, texel):
    positions = lax.broadcasted_iota(jnp.int32, (texel_taps.shape[1], texel), 1)
    matrix = jnp.zeros((texel_taps.shape[1], texel), jnp.float32)
    for number in range(4):
        matrix = matrix + jnp.where(
            texel_taps[number][:, None] == positions, weights[number][:, None], jnp.float32(0.0)
        )
    return matrix.astype(jnp.bfloat16)


def shifted(picture, shift_y, shift_x):
    height = picture.shape[1]
    width = picture.shape[2]
    padded_input = jnp.pad(picture, ((0, 0), (1, 1), (1, 1)))
    return padded_input[:, 1 + shift_y : 1 + shift_y + height, 1 + shift_x : 1 + shift_x + width]


def render_one(fetched, slot_row, cell_row, frac_row, conv_weight, cot_row):
    visible = fetched.shape[0]
    channels = fetched.shape[1]
    texel = fetched.shape[2]
    side = math.isqrt(texel)
    height = slot_row.shape[0]
    width = cell_row.shape[0] // height
    group_size = math.gcd(height, 16)
    group_count = height // group_size
    texel_taps, weights = taps_and_weights(cell_row, frac_row, side)
    taps_grouped = texel_taps.reshape(4, group_count, group_size * width).transpose(1, 0, 2)
    weights_grouped = weights.reshape(4, group_count, group_size * width).transpose(1, 0, 2)
    slots_grouped = slot_row.reshape(group_count, group_size)

    def forward(inputs):
        taps_part, weights_part, slots_part = inputs
        texture_lookup = sample_matrix(taps_part, weights_part, texel).reshape(
            group_size, width, texel
        )
        selected_entries = jnp.take(fetched, slots_part, axis=0)
        feature_maps = jnp.einsum(
            "qfm,qzm->qfz", selected_entries, texture_lookup, preferred_element_type=jnp.float32
        )
        return feature_maps.astype(jnp.bfloat16)

    grouped_features = lax.map(forward, (taps_grouped, weights_grouped, slots_grouped))
    feature_maps = grouped_features.transpose(2, 0, 1, 3).reshape(channels, height, width)
    offsets = [(shift_y, shift_x) for shift_y in (-1, 0, 1) for shift_x in (-1, 0, 1)]
    columns = jnp.concatenate(
        [shifted(feature_maps, shift_y, shift_x) for shift_y, shift_x in offsets], axis=0
    )
    columns = columns.reshape(9 * channels, height * width)
    preact = jnp.dot(conv_weight, columns, preferred_element_type=jnp.float32)
    sigmoid_pre = jax.nn.sigmoid(preact)
    rendered = (preact * sigmoid_pre).astype(jnp.bfloat16)
    pre_grad = (
        cot_row.astype(jnp.float32) * sigmoid_pre * (1.0 + preact * (1.0 - sigmoid_pre))
    ).astype(jnp.bfloat16)
    weight_local = jnp.einsum("op,kp->ok", pre_grad, columns, preferred_element_type=jnp.float32)
    col_grad = jnp.einsum("ok,op->kp", conv_weight, pre_grad, preferred_element_type=jnp.float32)
    col_grad = col_grad.reshape(9, channels, height, width)
    feat_grad = jnp.zeros((channels, height, width), jnp.float32)
    for number in range(9):
        shift_y, shift_x = offsets[number]
        feat_grad = feat_grad + shifted(col_grad[number], -shift_y, -shift_x)
    feat_grad = feat_grad.astype(jnp.bfloat16)
    grad_grouped = feat_grad.reshape(channels, group_count, group_size, width).transpose(1, 2, 0, 3)
    slot_numbers = jnp.arange(visible, dtype=jnp.int32)

    def backward(totals, inputs):
        taps_part, weights_part, slots_part, gradient_portion = inputs
        texture_lookup = sample_matrix(taps_part, weights_part, texel).reshape(
            group_size, width, texel
        )
        texel_gradient = jnp.einsum(
            "rzs,rsu->rzu", gradient_portion, texture_lookup, preferred_element_type=jnp.float32
        )
        selector = (slots_part[:, None] == slot_numbers[None, :]).astype(jnp.float32)
        added = jnp.einsum("gv,gct->vct", selector, texel_gradient, precision=lax.Precision.HIGHEST)
        return (totals + added, None)

    start = jnp.zeros((visible, channels, texel), jnp.float32)
    slot_grad, unused = lax.scan(
        backward, start, (taps_grouped, weights_grouped, slots_grouped, grad_grouped)
    )
    return (rendered, slot_grad.reshape(visible, channels * texel), weight_local)


def render_flat(fetched, slot_row, lookup, conv_weight, cot_row):
    visible = fetched.shape[0]
    channels = fetched.shape[1]
    texel = fetched.shape[2]
    height = slot_row.shape[0]
    width = lookup.shape[1]
    selected_entries = jnp.take(fetched, slot_row, axis=0, mode="clip")
    feature_maps = jnp.einsum(
        "qfm,qzm->fqz", selected_entries, lookup, preferred_element_type=jnp.float32
    ).astype(jnp.bfloat16)
    offsets = [(shift_y, shift_x) for shift_y in (-1, 0, 1) for shift_x in (-1, 0, 1)]
    columns = jnp.concatenate(
        [shifted(feature_maps, shift_y, shift_x) for shift_y, shift_x in offsets], axis=0
    )
    columns = columns.reshape(9 * channels, height * width)
    preact = jnp.dot(conv_weight, columns, preferred_element_type=jnp.float32)
    sigmoid_pre = jax.nn.sigmoid(preact)
    rendered = (preact * sigmoid_pre).astype(jnp.bfloat16)
    pre_grad = (
        cot_row.astype(jnp.float32) * sigmoid_pre * (1.0 + preact * (1.0 - sigmoid_pre))
    ).astype(jnp.bfloat16)
    weight_local = jnp.einsum("op,kp->ok", pre_grad, columns, preferred_element_type=jnp.float32)
    col_grad = jnp.einsum("ok,op->kp", conv_weight, pre_grad, preferred_element_type=jnp.float32)
    col_grad = col_grad.reshape(9, channels, height, width)
    feat_grad = jnp.zeros((channels, height, width), jnp.float32)
    for number in range(9):
        shift_y, shift_x = offsets[number]
        feat_grad = feat_grad + shifted(col_grad[number], -shift_y, -shift_x)
    feat_grad = feat_grad.astype(jnp.bfloat16)
    texel_gradient = jnp.einsum(
        "zrs,rsu->rzu", feat_grad, lookup, preferred_element_type=jnp.float32
    )
    slot_numbers = jnp.arange(visible, dtype=jnp.int32)
    selector = (slot_row[:, None] == slot_numbers[None, :]).astype(jnp.float32)
    slot_grad = jnp.einsum(
        "gv,gct->vct", selector, texel_gradient, precision=lax.Precision.HIGHEST
    )
    return (rendered, slot_grad.reshape(visible, channels * texel), weight_local)


def per_device(texture, requests, block_slot, texel_cell, uv_frac, conv_weight, cotangent):
    owners = lax.axis_size("tex")
    frame_count = lax.axis_size("frames")
    tile_count = texture.shape[0]
    tile_width = texture.shape[1]
    texel = tile_width // CH
    height = block_slot.shape[1]
    texel_taps, weights = taps_and_weights(texel_cell[0], uv_frac[0], math.isqrt(texel))
    lookup = sample_matrix(texel_taps, weights, texel).reshape(height, -1, texel)
    wanted_ids = requests.reshape(owners, -1)
    wanted = lax.all_to_all(wanted_ids, "tex", split_axis=0, concat_axis=0, tiled=True)
    lookup, wanted = lax.optimization_barrier((lookup, wanted))
    per_owner = wanted.shape[1]
    visible = owners * per_owner
    served = jnp.take(
        texture.reshape(tile_count, CH, texel), wanted.reshape(-1), axis=0, mode="clip"
    ).reshape(owners, per_owner * CH, texel)
    fetched = lax.all_to_all(served, "tex", split_axis=0, concat_axis=0, tiled=True)
    fetched = fetched.reshape(visible, CH, texel)
    rendered, slot_grad, weight_local = render_flat(
        fetched, block_slot[0], lookup, conv_weight, cotangent[0]
    )
    columns = tile_width // frame_count
    weight_size = weight_local.size
    chunk = -(-weight_size // frame_count)
    request_count = requests.shape[1]
    weight_rows = jnp.pad(weight_local.reshape(-1), (0, chunk * frame_count - weight_size))
    weight_rows = weight_rows.reshape(frame_count, chunk)
    weight_high = weight_rows.astype(jnp.bfloat16)
    weight_low = (weight_rows - weight_high.astype(jnp.float32)).astype(jnp.bfloat16)
    extra = -(-(2 * chunk + request_count) // columns)
    side_row = jnp.concatenate(
        [
            weight_high,
            weight_low,
            jnp.broadcast_to(requests.astype(jnp.bfloat16), (frame_count, request_count)),
            jnp.zeros((frame_count, extra * columns - 2 * chunk - request_count), jnp.bfloat16),
        ],
        axis=1,
    ).reshape(frame_count, extra, columns)
    spread = slot_grad.reshape(visible, frame_count, columns).transpose(1, 0, 2)
    spread = jnp.concatenate([spread.astype(jnp.bfloat16), side_row], axis=1)
    gathered = lax.all_to_all(spread, "frames", split_axis=0, concat_axis=0, tiled=True)
    side = gathered[:, visible:].reshape(frame_count, extra * columns).astype(jnp.float32)
    frame_weight = jnp.sum(side[:, :chunk] + side[:, chunk : 2 * chunk], axis=0)
    senders = side[:, 2 * chunk : 2 * chunk + request_count].astype(jnp.int32)
    senders = senders.reshape(frame_count, owners, per_owner)
    gathered = gathered[:, :visible].astype(jnp.float32)
    gathered = gathered.reshape(frame_count, owners, per_owner, columns)
    tile_numbers = jnp.arange(tile_count, dtype=jnp.int32)
    selector = (senders[None] == tile_numbers[:, None, None, None]).astype(jnp.float32)
    partial = jnp.einsum(
        "qfoj,fojc->oqc", selector, gathered, precision=lax.Precision.HIGHEST
    )
    weight_high = frame_weight.astype(jnp.bfloat16)
    weight_low = (frame_weight - weight_high.astype(jnp.float32)).astype(jnp.bfloat16)
    weight_tail = -(-(2 * chunk) // columns) * columns
    weight_block = jnp.pad(
        jnp.concatenate([weight_high, weight_low]), (0, weight_tail - 2 * chunk)
    ).reshape(1, -1, columns)
    partial = jnp.concatenate(
        [
            partial.astype(jnp.bfloat16),
            jnp.broadcast_to(weight_block, (owners,) + weight_block.shape[1:]),
        ],
        axis=1,
    )
    received = lax.all_to_all(partial, "tex", 0, 0, tiled=True).astype(jnp.float32)
    collected = jnp.sum(received, axis=0)
    texture_grad = collected[:tile_count]
    weight_pair = collected[tile_count:].reshape(-1)
    chunk_total = weight_pair[:chunk] + weight_pair[chunk : 2 * chunk]
    shared = lax.all_to_all(
        jnp.broadcast_to(chunk_total[None], (frame_count, chunk)), "frames", 0, 0, tiled=True
    )
    norm_scale = 1.0 / math.sqrt(frame_count * owners * cotangent.shape[2])
    weight_grad = shared.reshape(-1)[:weight_size].reshape(weight_local.shape) * norm_scale
    return (rendered[None], texture_grad, weight_grad)


def solution(mesh):
    placed = (
        P("tex", None),
        P(("frames", "tex"), None),
        P(("frames", "tex"), None),
        P(("frames", "tex"), None),
        P(("frames", "tex"), None, None),
        P(),
        P(("frames", "tex"), None, None),
    )
    return jax.shard_map(
        per_device,
        mesh=mesh,
        in_specs=placed,
        out_specs=(P(("frames", "tex"), None, None), P("tex", "frames"), P()),
        check_vma=False,
    )
```

```python
import math

import jax
import jax.numpy as jnp
from jax import lax
from jax.sharding import PartitionSpec as P

CH = 16
LANE = 128


def taps_and_weights(cell_row, frac_row, side):
    column = cell_row % (side - 1)
    row_index = cell_row // (side - 1)
    corner = row_index * side + column
    texel_taps = jnp.stack([corner, corner + 1, corner + side, corner + side + 1])
    frac_x = frac_row[0]
    frac_y = frac_row[1]
    weights = jnp.stack(
        [
            (1.0 - frac_x) * (1.0 - frac_y),
            frac_x * (1.0 - frac_y),
            (1.0 - frac_x) * frac_y,
            frac_x * frac_y,
        ]
    )
    return (texel_taps, weights)


def sample_matrix(texel_taps, weights, texel):
    positions = lax.broadcasted_iota(jnp.int32, (texel_taps.shape[1], texel), 1)
    matrix = jnp.zeros((texel_taps.shape[1], texel), jnp.float32)
    for number in range(4):
        matrix = matrix + jnp.where(
            texel_taps[number][:, None] == positions, weights[number][:, None], jnp.float32(0.0)
        )
    return matrix.astype(jnp.bfloat16)


def shifted(picture, shift_y, shift_x):
    height = picture.shape[1]
    width = picture.shape[2]
    padded_input = jnp.pad(picture, ((0, 0), (1, 1), (1, 1)))
    return padded_input[:, 1 + shift_y : 1 + shift_y + height, 1 + shift_x : 1 + shift_x + width]


def render_one(fetched, slot_row, cell_row, frac_row, conv_weight, cot_row):
    visible = fetched.shape[0]
    channels = fetched.shape[1]
    texel = fetched.shape[2]
    side = math.isqrt(texel)
    height = slot_row.shape[0]
    width = cell_row.shape[0] // height
    group_size = math.gcd(height, 16)
    group_count = height // group_size
    texel_taps, weights = taps_and_weights(cell_row, frac_row, side)
    taps_grouped = texel_taps.reshape(4, group_count, group_size * width).transpose(1, 0, 2)
    weights_grouped = weights.reshape(4, group_count, group_size * width).transpose(1, 0, 2)
    slots_grouped = slot_row.reshape(group_count, group_size)

    def forward(inputs):
        taps_part, weights_part, slots_part = inputs
        texture_lookup = sample_matrix(taps_part, weights_part, texel).reshape(
            group_size, width, texel
        )
        selected_entries = jnp.take(fetched, slots_part, axis=0)
        feature_maps = jnp.einsum(
            "qfm,qzm->qfz", selected_entries, texture_lookup, preferred_element_type=jnp.float32
        )
        return feature_maps.astype(jnp.bfloat16)

    grouped_features = lax.map(forward, (taps_grouped, weights_grouped, slots_grouped))
    feature_maps = grouped_features.transpose(2, 0, 1, 3).reshape(channels, height, width)
    offsets = [(shift_y, shift_x) for shift_y in (-1, 0, 1) for shift_x in (-1, 0, 1)]
    columns = jnp.concatenate(
        [shifted(feature_maps, shift_y, shift_x) for shift_y, shift_x in offsets], axis=0
    )
    columns = columns.reshape(9 * channels, height * width)
    preact = jnp.dot(conv_weight, columns, preferred_element_type=jnp.float32)
    sigmoid_pre = jax.nn.sigmoid(preact)
    rendered = (preact * sigmoid_pre).astype(jnp.bfloat16)
    pre_grad = (
        cot_row.astype(jnp.float32) * sigmoid_pre * (1.0 + preact * (1.0 - sigmoid_pre))
    ).astype(jnp.bfloat16)
    weight_local = jnp.einsum("op,kp->ok", pre_grad, columns, preferred_element_type=jnp.float32)
    col_grad = jnp.einsum("ok,op->kp", conv_weight, pre_grad, preferred_element_type=jnp.float32)
    col_grad = col_grad.reshape(9, channels, height, width)
    feat_grad = jnp.zeros((channels, height, width), jnp.float32)
    for number in range(9):
        shift_y, shift_x = offsets[number]
        feat_grad = feat_grad + shifted(col_grad[number], -shift_y, -shift_x)
    feat_grad = feat_grad.astype(jnp.bfloat16)
    grad_grouped = feat_grad.reshape(channels, group_count, group_size, width).transpose(1, 2, 0, 3)
    slot_numbers = jnp.arange(visible, dtype=jnp.int32)

    def backward(totals, inputs):
        taps_part, weights_part, slots_part, gradient_portion = inputs
        texture_lookup = sample_matrix(taps_part, weights_part, texel).reshape(
            group_size, width, texel
        )
        texel_gradient = jnp.einsum(
            "rzs,rsu->rzu", gradient_portion, texture_lookup, preferred_element_type=jnp.float32
        )
        selector = (slots_part[:, None] == slot_numbers[None, :]).astype(jnp.float32)
        added = jnp.einsum("gv,gct->vct", selector, texel_gradient, precision=lax.Precision.HIGHEST)
        return (totals + added, None)

    start = jnp.zeros((visible, channels, texel), jnp.float32)
    slot_grad, unused = lax.scan(
        backward, start, (taps_grouped, weights_grouped, slots_grouped, grad_grouped)
    )
    return (rendered, slot_grad.reshape(visible, channels * texel), weight_local)


def render_flat(fetched, slot_row, lookup, conv_weight, cot_row):
    visible = fetched.shape[0]
    channels = fetched.shape[1]
    texel = fetched.shape[2]
    height = slot_row.shape[0]
    width = lookup.shape[1]
    selected_entries = jnp.take(fetched, slot_row, axis=0, mode="clip")
    feature_maps = jnp.einsum(
        "qfm,qzm->fqz", selected_entries, lookup, preferred_element_type=jnp.float32
    ).astype(jnp.bfloat16)
    offsets = [(shift_y, shift_x) for shift_y in (-1, 0, 1) for shift_x in (-1, 0, 1)]
    columns = jnp.concatenate(
        [shifted(feature_maps, shift_y, shift_x) for shift_y, shift_x in offsets], axis=0
    )
    columns = columns.reshape(9 * channels, height * width)
    preact = jnp.dot(conv_weight, columns, preferred_element_type=jnp.float32)
    sigmoid_pre = jax.nn.sigmoid(preact)
    rendered = (preact * sigmoid_pre).astype(jnp.bfloat16)
    pre_grad = (
        cot_row.astype(jnp.float32) * sigmoid_pre * (1.0 + preact * (1.0 - sigmoid_pre))
    ).astype(jnp.bfloat16)
    weight_local = jnp.einsum("op,kp->ok", pre_grad, columns, preferred_element_type=jnp.float32)
    col_grad = jnp.einsum("ok,op->kp", conv_weight, pre_grad, preferred_element_type=jnp.float32)
    col_grad = col_grad.reshape(9, channels, height, width)
    feat_grad = jnp.zeros((channels, height, width), jnp.float32)
    for number in range(9):
        shift_y, shift_x = offsets[number]
        feat_grad = feat_grad + shifted(col_grad[number], -shift_y, -shift_x)
    feat_grad = feat_grad.astype(jnp.bfloat16)
    texel_gradient = jnp.einsum(
        "zrs,rsu->rzu", feat_grad, lookup, preferred_element_type=jnp.float32
    )
    slot_numbers = jnp.arange(visible, dtype=jnp.int32)
    selector = (slot_row[:, None] == slot_numbers[None, :]).astype(jnp.float32)
    slot_grad = jnp.einsum(
        "gv,gct->vct", selector, texel_gradient, precision=lax.Precision.HIGHEST
    )
    return (rendered, slot_grad.reshape(visible, channels * texel), weight_local)


def per_device(texture, requests, block_slot, texel_cell, uv_frac, conv_weight, cotangent):
    owners = lax.axis_size("tex")
    frame_count = lax.axis_size("frames")
    tile_count = texture.shape[0]
    tile_width = texture.shape[1]
    texel = tile_width // CH
    height = block_slot.shape[1]
    texel_taps, weights = taps_and_weights(texel_cell[0], uv_frac[0], math.isqrt(texel))
    lookup = sample_matrix(texel_taps, weights, texel).reshape(height, -1, texel)
    lookup = lax.optimization_barrier(lookup)
    wanted_ids = requests.reshape(owners, -1)
    wanted = lax.all_to_all(wanted_ids, "tex", split_axis=0, concat_axis=0, tiled=True)
    per_owner = wanted.shape[1]
    visible = owners * per_owner
    served = jnp.take(
        texture.reshape(tile_count, CH, texel), wanted.reshape(-1), axis=0, mode="clip"
    ).reshape(owners, per_owner * CH, texel)
    fetched = lax.all_to_all(served, "tex", split_axis=0, concat_axis=0, tiled=True)
    fetched = fetched.reshape(visible, CH, texel)
    rendered, slot_grad, weight_local = render_flat(
        fetched, block_slot[0], lookup, conv_weight, cotangent[0]
    )
    columns = tile_width // frame_count
    weight_size = weight_local.size
    chunk = -(-weight_size // frame_count)
    request_count = requests.shape[1]
    weight_rows = jnp.pad(weight_local.reshape(-1), (0, chunk * frame_count - weight_size))
    weight_rows = weight_rows.reshape(frame_count, chunk)
    weight_high = weight_rows.astype(jnp.bfloat16)
    weight_low = (weight_rows - weight_high.astype(jnp.float32)).astype(jnp.bfloat16)
    extra = -(-(2 * chunk + request_count) // columns)
    side_row = jnp.concatenate(
        [
            weight_high,
            weight_low,
            jnp.broadcast_to(requests.astype(jnp.bfloat16), (frame_count, request_count)),
            jnp.zeros((frame_count, extra * columns - 2 * chunk - request_count), jnp.bfloat16),
        ],
        axis=1,
    ).reshape(frame_count, extra * columns // LANE, LANE)
    spread = slot_grad.reshape(visible, frame_count, columns).transpose(1, 0, 2)
    spread = spread.astype(jnp.bfloat16).reshape(frame_count, visible * columns // LANE, LANE)
    spread = jnp.concatenate([spread, side_row], axis=1)
    gathered = lax.all_to_all(spread, "frames", split_axis=0, concat_axis=0, tiled=True)
    grad_rows = visible * columns // LANE
    side = gathered[:, grad_rows:].reshape(frame_count, extra * columns).astype(jnp.float32)
    frame_weight = jnp.sum(side[:, :chunk] + side[:, chunk : 2 * chunk], axis=0)
    senders = side[:, 2 * chunk : 2 * chunk + request_count].astype(jnp.int32)
    senders = senders.reshape(frame_count, owners, per_owner)
    gathered = gathered[:, :grad_rows].astype(jnp.float32)
    gathered = gathered.reshape(frame_count, owners, per_owner, columns)
    tile_numbers = jnp.arange(tile_count, dtype=jnp.int32)
    selector = (senders[None] == tile_numbers[:, None, None, None]).astype(jnp.float32)
    partial = jnp.einsum(
        "qfoj,fojc->oqc", selector, gathered, precision=lax.Precision.HIGHEST
    )
    weight_high = frame_weight.astype(jnp.bfloat16)
    weight_low = (frame_weight - weight_high.astype(jnp.float32)).astype(jnp.bfloat16)
    weight_tail = -(-(2 * chunk) // columns) * columns
    weight_block = jnp.pad(
        jnp.concatenate([weight_high, weight_low]), (0, weight_tail - 2 * chunk)
    ).reshape(1, -1, LANE)
    partial = jnp.concatenate(
        [
            partial.astype(jnp.bfloat16).reshape(owners, tile_count * columns // LANE, LANE),
            jnp.broadcast_to(weight_block, (owners,) + weight_block.shape[1:]),
        ],
        axis=1,
    )
    received = lax.all_to_all(partial, "tex", 0, 0, tiled=True).astype(jnp.float32)
    collected = jnp.sum(received, axis=0)
    tile_rows = tile_count * columns // LANE
    texture_grad = collected[:tile_rows].reshape(tile_count, columns)
    weight_pair = collected[tile_rows:].reshape(-1)
    chunk_total = weight_pair[:chunk] + weight_pair[chunk : 2 * chunk]
    shared = lax.all_to_all(
        jnp.broadcast_to(chunk_total[None], (frame_count, chunk)), "frames", 0, 0, tiled=True
    )
    norm_scale = 1.0 / math.sqrt(frame_count * owners * cotangent.shape[2])
    weight_grad = shared.reshape(-1)[:weight_size].reshape(weight_local.shape) * norm_scale
    return (rendered[None], texture_grad, weight_grad)


def solution(mesh):
    placed = (
        P("tex", None),
        P(("frames", "tex"), None),
        P(("frames", "tex"), None),
        P(("frames", "tex"), None),
        P(("frames", "tex"), None, None),
        P(),
        P(("frames", "tex"), None, None),
    )
    return jax.shard_map(
        per_device,
        mesh=mesh,
        in_specs=placed,
        out_specs=(P(("frames", "tex"), None, None), P("tex", "frames"), P()),
        check_vma=False,
    )
```

```python
import math

import jax
import jax.numpy as jnp
from jax import lax
from jax.sharding import PartitionSpec as P

CH = 16
LANE = 128


def taps_and_weights(cell_row, frac_row, side):
    column = cell_row % (side - 1)
    row_index = cell_row // (side - 1)
    corner = row_index * side + column
    texel_taps = jnp.stack([corner, corner + 1, corner + side, corner + side + 1])
    frac_x = frac_row[0]
    frac_y = frac_row[1]
    weights = jnp.stack(
        [
            (1.0 - frac_x) * (1.0 - frac_y),
            frac_x * (1.0 - frac_y),
            (1.0 - frac_x) * frac_y,
            frac_x * frac_y,
        ]
    )
    return (texel_taps, weights)


def sample_matrix(texel_taps, weights, texel):
    positions = lax.broadcasted_iota(jnp.int32, (texel_taps.shape[1], texel), 1)
    matrix = jnp.zeros((texel_taps.shape[1], texel), jnp.float32)
    for number in range(4):
        matrix = matrix + jnp.where(
            texel_taps[number][:, None] == positions, weights[number][:, None], jnp.float32(0.0)
        )
    return matrix.astype(jnp.bfloat16)


def shifted(picture, shift_y, shift_x):
    height = picture.shape[1]
    width = picture.shape[2]
    padded_input = jnp.pad(picture, ((0, 0), (1, 1), (1, 1)))
    return padded_input[:, 1 + shift_y : 1 + shift_y + height, 1 + shift_x : 1 + shift_x + width]


def render_one(fetched, slot_row, cell_row, frac_row, conv_weight, cot_row):
    visible = fetched.shape[0]
    channels = fetched.shape[1]
    texel = fetched.shape[2]
    side = math.isqrt(texel)
    height = slot_row.shape[0]
    width = cell_row.shape[0] // height
    group_size = math.gcd(height, 16)
    group_count = height // group_size
    texel_taps, weights = taps_and_weights(cell_row, frac_row, side)
    taps_grouped = texel_taps.reshape(4, group_count, group_size * width).transpose(1, 0, 2)
    weights_grouped = weights.reshape(4, group_count, group_size * width).transpose(1, 0, 2)
    slots_grouped = slot_row.reshape(group_count, group_size)

    def forward(inputs):
        taps_part, weights_part, slots_part = inputs
        texture_lookup = sample_matrix(taps_part, weights_part, texel).reshape(
            group_size, width, texel
        )
        selected_entries = jnp.take(fetched, slots_part, axis=0)
        feature_maps = jnp.einsum(
            "qfm,qzm->qfz", selected_entries, texture_lookup, preferred_element_type=jnp.float32
        )
        return feature_maps.astype(jnp.bfloat16)

    grouped_features = lax.map(forward, (taps_grouped, weights_grouped, slots_grouped))
    feature_maps = grouped_features.transpose(2, 0, 1, 3).reshape(channels, height, width)
    offsets = [(shift_y, shift_x) for shift_y in (-1, 0, 1) for shift_x in (-1, 0, 1)]
    columns = jnp.concatenate(
        [shifted(feature_maps, shift_y, shift_x) for shift_y, shift_x in offsets], axis=0
    )
    columns = columns.reshape(9 * channels, height * width)
    preact = jnp.dot(conv_weight, columns, preferred_element_type=jnp.float32)
    sigmoid_pre = jax.nn.sigmoid(preact)
    rendered = (preact * sigmoid_pre).astype(jnp.bfloat16)
    pre_grad = (
        cot_row.astype(jnp.float32) * sigmoid_pre * (1.0 + preact * (1.0 - sigmoid_pre))
    ).astype(jnp.bfloat16)
    weight_local = jnp.einsum("op,kp->ok", pre_grad, columns, preferred_element_type=jnp.float32)
    col_grad = jnp.einsum("ok,op->kp", conv_weight, pre_grad, preferred_element_type=jnp.float32)
    col_grad = col_grad.reshape(9, channels, height, width)
    feat_grad = jnp.zeros((channels, height, width), jnp.float32)
    for number in range(9):
        shift_y, shift_x = offsets[number]
        feat_grad = feat_grad + shifted(col_grad[number], -shift_y, -shift_x)
    feat_grad = feat_grad.astype(jnp.bfloat16)
    grad_grouped = feat_grad.reshape(channels, group_count, group_size, width).transpose(1, 2, 0, 3)
    slot_numbers = jnp.arange(visible, dtype=jnp.int32)

    def backward(totals, inputs):
        taps_part, weights_part, slots_part, gradient_portion = inputs
        texture_lookup = sample_matrix(taps_part, weights_part, texel).reshape(
            group_size, width, texel
        )
        texel_gradient = jnp.einsum(
            "rzs,rsu->rzu", gradient_portion, texture_lookup, preferred_element_type=jnp.float32
        )
        selector = (slots_part[:, None] == slot_numbers[None, :]).astype(jnp.float32)
        added = jnp.einsum("gv,gct->vct", selector, texel_gradient, precision=lax.Precision.HIGHEST)
        return (totals + added, None)

    start = jnp.zeros((visible, channels, texel), jnp.float32)
    slot_grad, unused = lax.scan(
        backward, start, (taps_grouped, weights_grouped, slots_grouped, grad_grouped)
    )
    return (rendered, slot_grad.reshape(visible, channels * texel), weight_local)


def render_flat(fetched, slot_row, lookup, conv_weight, cot_row):
    visible = fetched.shape[0]
    channels = fetched.shape[1]
    texel = fetched.shape[2]
    height = slot_row.shape[0]
    width = lookup.shape[1]
    selected_entries = jnp.take(fetched, slot_row, axis=0, mode="clip")
    feature_maps = jnp.einsum(
        "qfm,qzm->fqz", selected_entries, lookup, preferred_element_type=jnp.float32
    ).astype(jnp.bfloat16)
    offsets = [(shift_y, shift_x) for shift_y in (-1, 0, 1) for shift_x in (-1, 0, 1)]
    columns = jnp.concatenate(
        [shifted(feature_maps, shift_y, shift_x) for shift_y, shift_x in offsets], axis=0
    )
    columns = columns.reshape(9 * channels, height * width)
    preact = jnp.dot(conv_weight, columns, preferred_element_type=jnp.float32)
    sigmoid_pre = jax.nn.sigmoid(preact)
    rendered = (preact * sigmoid_pre).astype(jnp.bfloat16)
    pre_grad = (
        cot_row.astype(jnp.float32) * sigmoid_pre * (1.0 + preact * (1.0 - sigmoid_pre))
    ).astype(jnp.bfloat16)
    weight_local = jnp.einsum("op,kp->ok", pre_grad, columns, preferred_element_type=jnp.float32)
    col_grad = jnp.einsum("ok,op->kp", conv_weight, pre_grad, preferred_element_type=jnp.float32)
    col_grad = col_grad.reshape(9, channels, height, width)
    feat_grad = jnp.zeros((channels, height, width), jnp.float32)
    for number in range(9):
        shift_y, shift_x = offsets[number]
        feat_grad = feat_grad + shifted(col_grad[number], -shift_y, -shift_x)
    feat_grad = feat_grad.astype(jnp.bfloat16)
    slot_numbers = jnp.arange(visible, dtype=jnp.int32)
    selector = (slot_numbers[:, None] == slot_row[None, :]).astype(jnp.bfloat16)
    routed = selector[:, None, :, None] * feat_grad[None]
    slot_grad = jnp.einsum(
        "vcrs,rsu->vcu", routed, lookup, preferred_element_type=jnp.float32
    )
    return (rendered, slot_grad.reshape(visible, channels * texel), weight_local)


def per_device(texture, requests, block_slot, texel_cell, uv_frac, conv_weight, cotangent):
    owners = lax.axis_size("tex")
    frame_count = lax.axis_size("frames")
    tile_count = texture.shape[0]
    tile_width = texture.shape[1]
    texel = tile_width // CH
    height = block_slot.shape[1]
    texel_taps, weights = taps_and_weights(texel_cell[0], uv_frac[0], math.isqrt(texel))
    lookup = sample_matrix(texel_taps, weights, texel).reshape(height, -1, texel)
    lookup = lax.optimization_barrier(lookup)
    wanted_ids = requests.reshape(owners, -1)
    wanted = lax.all_to_all(wanted_ids, "tex", split_axis=0, concat_axis=0, tiled=True)
    per_owner = wanted.shape[1]
    visible = owners * per_owner
    served = jnp.take(
        texture.reshape(tile_count, CH, texel), wanted.reshape(-1), axis=0, mode="clip"
    ).reshape(owners, per_owner * CH, texel)
    fetched = lax.all_to_all(served, "tex", split_axis=0, concat_axis=0, tiled=True)
    fetched = fetched.reshape(visible, CH, texel)
    rendered, slot_grad, weight_local = render_flat(
        fetched, block_slot[0], lookup, conv_weight, cotangent[0]
    )
    columns = tile_width // frame_count
    weight_size = weight_local.size
    chunk = -(-weight_size // frame_count)
    request_count = requests.shape[1]
    weight_rows = jnp.pad(weight_local.reshape(-1), (0, chunk * frame_count - weight_size))
    weight_rows = weight_rows.reshape(frame_count, chunk)
    weight_high = weight_rows.astype(jnp.bfloat16)
    weight_low = (weight_rows - weight_high.astype(jnp.float32)).astype(jnp.bfloat16)
    extra = -(-(2 * chunk + request_count) // columns)
    side_row = jnp.concatenate(
        [
            weight_high,
            weight_low,
            jnp.broadcast_to(requests.astype(jnp.bfloat16), (frame_count, request_count)),
            jnp.zeros((frame_count, extra * columns - 2 * chunk - request_count), jnp.bfloat16),
        ],
        axis=1,
    ).reshape(frame_count, extra * columns // LANE, LANE)
    spread = slot_grad.reshape(visible, frame_count, columns).transpose(1, 0, 2)
    spread = spread.astype(jnp.bfloat16).reshape(frame_count, visible * columns // LANE, LANE)
    spread = jnp.concatenate([spread, side_row], axis=1)
    gathered = lax.all_to_all(spread, "frames", split_axis=0, concat_axis=0, tiled=True)
    grad_rows = visible * columns // LANE
    side = gathered[:, grad_rows:].reshape(frame_count, extra * columns).astype(jnp.float32)
    frame_weight = jnp.sum(side[:, :chunk] + side[:, chunk : 2 * chunk], axis=0)
    senders = side[:, 2 * chunk : 2 * chunk + request_count].astype(jnp.int32)
    senders = senders.reshape(frame_count, owners, per_owner)
    gathered = gathered[:, :grad_rows].astype(jnp.float32)
    gathered = gathered.reshape(frame_count, owners, per_owner, columns)
    tile_numbers = jnp.arange(tile_count, dtype=jnp.int32)
    selector = (senders[None] == tile_numbers[:, None, None, None]).astype(jnp.float32)
    partial = jnp.einsum(
        "qfoj,fojc->oqc", selector, gathered, precision=lax.Precision.HIGHEST
    )
    weight_high = frame_weight.astype(jnp.bfloat16)
    weight_low = (frame_weight - weight_high.astype(jnp.float32)).astype(jnp.bfloat16)
    weight_tail = -(-(2 * chunk) // columns) * columns
    weight_block = jnp.pad(
        jnp.concatenate([weight_high, weight_low]), (0, weight_tail - 2 * chunk)
    ).reshape(1, -1, LANE)
    partial = jnp.concatenate(
        [
            partial.astype(jnp.bfloat16).reshape(owners, tile_count * columns // LANE, LANE),
            jnp.broadcast_to(weight_block, (owners,) + weight_block.shape[1:]),
        ],
        axis=1,
    )
    received = lax.all_to_all(partial, "tex", 0, 0, tiled=True).astype(jnp.float32)
    collected = jnp.sum(received, axis=0)
    tile_rows = tile_count * columns // LANE
    texture_grad = collected[:tile_rows].reshape(tile_count, columns)
    weight_pair = collected[tile_rows:].reshape(-1)
    chunk_total = weight_pair[:chunk] + weight_pair[chunk : 2 * chunk]
    shared = lax.all_to_all(
        jnp.broadcast_to(chunk_total[None], (frame_count, chunk)), "frames", 0, 0, tiled=True
    )
    norm_scale = 1.0 / math.sqrt(frame_count * owners * cotangent.shape[2])
    weight_grad = shared.reshape(-1)[:weight_size].reshape(weight_local.shape) * norm_scale
    return (rendered[None], texture_grad, weight_grad)


def solution(mesh):
    placed = (
        P("tex", None),
        P(("frames", "tex"), None),
        P(("frames", "tex"), None),
        P(("frames", "tex"), None),
        P(("frames", "tex"), None, None),
        P(),
        P(("frames", "tex"), None, None),
    )
    return jax.shard_map(
        per_device,
        mesh=mesh,
        in_specs=placed,
        out_specs=(P(("frames", "tex"), None, None), P("tex", "frames"), P()),
        check_vma=False,
    )
```

```python
import math

import jax
import jax.numpy as jnp
from jax import lax
from jax.sharding import PartitionSpec as P

CH = 16
LANE = 128


def taps_and_weights(cell_row, frac_row, side):
    column = cell_row % (side - 1)
    row_index = cell_row // (side - 1)
    corner = row_index * side + column
    texel_taps = jnp.stack([corner, corner + 1, corner + side, corner + side + 1])
    frac_x = frac_row[0]
    frac_y = frac_row[1]
    weights = jnp.stack(
        [
            (1.0 - frac_x) * (1.0 - frac_y),
            frac_x * (1.0 - frac_y),
            (1.0 - frac_x) * frac_y,
            frac_x * frac_y,
        ]
    )
    return (texel_taps, weights)


def sample_matrix(texel_taps, weights, texel):
    positions = lax.broadcasted_iota(jnp.int32, (texel_taps.shape[1], texel), 1)
    matrix = jnp.zeros((texel_taps.shape[1], texel), jnp.float32)
    for number in range(4):
        matrix = matrix + jnp.where(
            texel_taps[number][:, None] == positions, weights[number][:, None], jnp.float32(0.0)
        )
    return matrix.astype(jnp.bfloat16)


def shifted(picture, shift_y, shift_x):
    height = picture.shape[1]
    width = picture.shape[2]
    padded_input = jnp.pad(picture, ((0, 0), (1, 1), (1, 1)))
    return padded_input[:, 1 + shift_y : 1 + shift_y + height, 1 + shift_x : 1 + shift_x + width]


def render_one(fetched, slot_row, cell_row, frac_row, conv_weight, cot_row):
    visible = fetched.shape[0]
    channels = fetched.shape[1]
    texel = fetched.shape[2]
    side = math.isqrt(texel)
    height = slot_row.shape[0]
    width = cell_row.shape[0] // height
    group_size = math.gcd(height, 16)
    group_count = height // group_size
    texel_taps, weights = taps_and_weights(cell_row, frac_row, side)
    taps_grouped = texel_taps.reshape(4, group_count, group_size * width).transpose(1, 0, 2)
    weights_grouped = weights.reshape(4, group_count, group_size * width).transpose(1, 0, 2)
    slots_grouped = slot_row.reshape(group_count, group_size)

    def forward(inputs):
        taps_part, weights_part, slots_part = inputs
        texture_lookup = sample_matrix(taps_part, weights_part, texel).reshape(
            group_size, width, texel
        )
        selected_entries = jnp.take(fetched, slots_part, axis=0)
        feature_maps = jnp.einsum(
            "qfm,qzm->qfz", selected_entries, texture_lookup, preferred_element_type=jnp.float32
        )
        return feature_maps.astype(jnp.bfloat16)

    grouped_features = lax.map(forward, (taps_grouped, weights_grouped, slots_grouped))
    feature_maps = grouped_features.transpose(2, 0, 1, 3).reshape(channels, height, width)
    offsets = [(shift_y, shift_x) for shift_y in (-1, 0, 1) for shift_x in (-1, 0, 1)]
    columns = jnp.concatenate(
        [shifted(feature_maps, shift_y, shift_x) for shift_y, shift_x in offsets], axis=0
    )
    columns = columns.reshape(9 * channels, height * width)
    preact = jnp.dot(conv_weight, columns, preferred_element_type=jnp.float32)
    sigmoid_pre = jax.nn.sigmoid(preact)
    rendered = (preact * sigmoid_pre).astype(jnp.bfloat16)
    pre_grad = (
        cot_row.astype(jnp.float32) * sigmoid_pre * (1.0 + preact * (1.0 - sigmoid_pre))
    ).astype(jnp.bfloat16)
    weight_local = jnp.einsum("op,kp->ok", pre_grad, columns, preferred_element_type=jnp.float32)
    col_grad = jnp.einsum("ok,op->kp", conv_weight, pre_grad, preferred_element_type=jnp.float32)
    col_grad = col_grad.reshape(9, channels, height, width)
    feat_grad = jnp.zeros((channels, height, width), jnp.float32)
    for number in range(9):
        shift_y, shift_x = offsets[number]
        feat_grad = feat_grad + shifted(col_grad[number], -shift_y, -shift_x)
    feat_grad = feat_grad.astype(jnp.bfloat16)
    grad_grouped = feat_grad.reshape(channels, group_count, group_size, width).transpose(1, 2, 0, 3)
    slot_numbers = jnp.arange(visible, dtype=jnp.int32)

    def backward(totals, inputs):
        taps_part, weights_part, slots_part, gradient_portion = inputs
        texture_lookup = sample_matrix(taps_part, weights_part, texel).reshape(
            group_size, width, texel
        )
        texel_gradient = jnp.einsum(
            "rzs,rsu->rzu", gradient_portion, texture_lookup, preferred_element_type=jnp.float32
        )
        selector = (slots_part[:, None] == slot_numbers[None, :]).astype(jnp.float32)
        added = jnp.einsum("gv,gct->vct", selector, texel_gradient, precision=lax.Precision.HIGHEST)
        return (totals + added, None)

    start = jnp.zeros((visible, channels, texel), jnp.float32)
    slot_grad, unused = lax.scan(
        backward, start, (taps_grouped, weights_grouped, slots_grouped, grad_grouped)
    )
    return (rendered, slot_grad.reshape(visible, channels * texel), weight_local)


def render_flat(fetched, slot_row, lookup, conv_weight, cot_row):
    visible = fetched.shape[0]
    channels = fetched.shape[1]
    texel = fetched.shape[2]
    height = slot_row.shape[0]
    width = lookup.shape[1]
    selected_entries = jnp.take(fetched, slot_row, axis=0, mode="clip")
    feature_maps = jnp.einsum(
        "qfm,qzm->fqz", selected_entries, lookup, preferred_element_type=jnp.float32
    ).astype(jnp.bfloat16)
    offsets = [(shift_y, shift_x) for shift_y in (-1, 0, 1) for shift_x in (-1, 0, 1)]
    columns = jnp.concatenate(
        [shifted(feature_maps, shift_y, shift_x) for shift_y, shift_x in offsets], axis=0
    )
    columns = columns.reshape(9 * channels, height * width)
    preact = jnp.dot(conv_weight, columns, preferred_element_type=jnp.float32)
    sigmoid_pre = jax.nn.sigmoid(preact)
    rendered = (preact * sigmoid_pre).astype(jnp.bfloat16)
    pre_grad = (
        cot_row.astype(jnp.float32) * sigmoid_pre * (1.0 + preact * (1.0 - sigmoid_pre))
    ).astype(jnp.bfloat16)
    weight_local = jnp.einsum("op,kp->ok", pre_grad, columns, preferred_element_type=jnp.float32)
    col_grad = jnp.einsum("ok,op->kp", conv_weight, pre_grad, preferred_element_type=jnp.float32)
    col_grad = col_grad.reshape(9, channels, height, width)
    feat_grad = jnp.zeros((channels, height, width), jnp.float32)
    for number in range(9):
        shift_y, shift_x = offsets[number]
        feat_grad = feat_grad + shifted(col_grad[number], -shift_y, -shift_x)
    feat_grad = feat_grad.astype(jnp.bfloat16)
    texel_gradient = jnp.einsum(
        "zrs,rsu->rzu", feat_grad, lookup, preferred_element_type=jnp.float32
    )
    slot_numbers = jnp.arange(visible, dtype=jnp.int32)
    selector = (slot_row[:, None] == slot_numbers[None, :]).astype(jnp.float32)
    slot_grad = jnp.einsum(
        "gv,gct->vct", selector, texel_gradient, precision=lax.Precision.HIGHEST
    )
    return (rendered, slot_grad.reshape(visible, channels * texel), weight_local)


def per_device(texture, requests, block_slot, texel_cell, uv_frac, conv_weight, cotangent):
    owners = lax.axis_size("tex")
    frame_count = lax.axis_size("frames")
    tile_count = texture.shape[0]
    tile_width = texture.shape[1]
    texel = tile_width // CH
    height = block_slot.shape[1]
    texel_taps, weights = taps_and_weights(texel_cell[0], uv_frac[0], math.isqrt(texel))
    lookup = sample_matrix(texel_taps, weights, texel).reshape(height, -1, texel)
    lookup = lax.optimization_barrier(lookup)
    wanted_ids = requests.reshape(owners, -1)
    wanted = lax.all_to_all(wanted_ids, "tex", split_axis=0, concat_axis=0, tiled=True)
    per_owner = wanted.shape[1]
    visible = owners * per_owner
    served = jnp.take(
        texture.reshape(tile_count, CH, texel), wanted.reshape(-1), axis=0, mode="clip"
    ).reshape(owners, per_owner * CH, texel)
    fetched = lax.all_to_all(served, "tex", split_axis=0, concat_axis=0, tiled=True)
    fetched = fetched.reshape(visible, CH, texel)
    rendered, slot_grad, weight_local = render_flat(
        fetched, block_slot[0], lookup, conv_weight, cotangent[0]
    )
    columns = tile_width // frame_count
    weight_size = weight_local.size
    chunk = -(-weight_size // frame_count)
    request_count = requests.shape[1]
    weight_rows = jnp.pad(weight_local.reshape(-1), (0, chunk * frame_count - weight_size))
    weight_rows = weight_rows.reshape(frame_count, chunk)
    weight_high = weight_rows.astype(jnp.bfloat16)
    weight_low = (weight_rows - weight_high.astype(jnp.float32)).astype(jnp.bfloat16)
    extra = -(-(2 * chunk + request_count) // columns)
    side_row = jnp.concatenate(
        [
            weight_high,
            weight_low,
            jnp.broadcast_to(requests.astype(jnp.bfloat16), (frame_count, request_count)),
            jnp.zeros((frame_count, extra * columns - 2 * chunk - request_count), jnp.bfloat16),
        ],
        axis=1,
    ).reshape(frame_count, extra * columns // LANE, LANE)
    spread = slot_grad.reshape(visible, frame_count, columns).transpose(1, 0, 2)
    spread = spread.astype(jnp.bfloat16).reshape(frame_count, visible * columns // LANE, LANE)
    spread = jnp.concatenate([spread, side_row], axis=1)
    gathered = lax.all_to_all(spread, "frames", split_axis=0, concat_axis=0, tiled=True)
    grad_rows = visible * columns // LANE
    side = gathered[:, grad_rows:].reshape(frame_count, extra * columns).astype(jnp.float32)
    frame_weight = jnp.sum(side[:, :chunk] + side[:, chunk : 2 * chunk], axis=0)
    senders = side[:, 2 * chunk : 2 * chunk + request_count].astype(jnp.int32)
    senders = senders.reshape(frame_count, owners, per_owner)
    gathered = gathered[:, :grad_rows]
    gathered = gathered.reshape(frame_count, owners, per_owner, columns)
    tile_numbers = jnp.arange(tile_count, dtype=jnp.int32)
    selector = (senders[None] == tile_numbers[:, None, None, None]).astype(jnp.bfloat16)
    partial = jnp.einsum(
        "qfoj,fojc->oqc", selector, gathered, preferred_element_type=jnp.float32
    )
    weight_high = frame_weight.astype(jnp.bfloat16)
    weight_low = (frame_weight - weight_high.astype(jnp.float32)).astype(jnp.bfloat16)
    weight_tail = -(-(2 * chunk) // columns) * columns
    weight_block = jnp.pad(
        jnp.concatenate([weight_high, weight_low]), (0, weight_tail - 2 * chunk)
    ).reshape(1, -1, LANE)
    partial = jnp.concatenate(
        [
            partial.astype(jnp.bfloat16).reshape(owners, tile_count * columns // LANE, LANE),
            jnp.broadcast_to(weight_block, (owners,) + weight_block.shape[1:]),
        ],
        axis=1,
    )
    received = lax.all_to_all(partial, "tex", 0, 0, tiled=True).astype(jnp.float32)
    collected = jnp.sum(received, axis=0)
    tile_rows = tile_count * columns // LANE
    texture_grad = collected[:tile_rows].reshape(tile_count, columns)
    weight_pair = collected[tile_rows:].reshape(-1)
    chunk_total = weight_pair[:chunk] + weight_pair[chunk : 2 * chunk]
    shared = lax.all_to_all(
        jnp.broadcast_to(chunk_total[None], (frame_count, chunk)), "frames", 0, 0, tiled=True
    )
    norm_scale = 1.0 / math.sqrt(frame_count * owners * cotangent.shape[2])
    weight_grad = shared.reshape(-1)[:weight_size].reshape(weight_local.shape) * norm_scale
    return (rendered[None], texture_grad, weight_grad)


def solution(mesh):
    placed = (
        P("tex", None),
        P(("frames", "tex"), None),
        P(("frames", "tex"), None),
        P(("frames", "tex"), None),
        P(("frames", "tex"), None, None),
        P(),
        P(("frames", "tex"), None, None),
    )
    return jax.shard_map(
        per_device,
        mesh=mesh,
        in_specs=placed,
        out_specs=(P(("frames", "tex"), None, None), P("tex", "frames"), P()),
        check_vma=False,
    )
```

```python
import math

import jax
import jax.numpy as jnp
from jax import lax
from jax.sharding import PartitionSpec as P

CH = 16
LANE = 128


def taps_and_weights(cell_row, frac_row, side):
    column = cell_row % (side - 1)
    row_index = cell_row // (side - 1)
    corner = row_index * side + column
    texel_taps = jnp.stack([corner, corner + 1, corner + side, corner + side + 1])
    frac_x = frac_row[0]
    frac_y = frac_row[1]
    weights = jnp.stack(
        [
            (1.0 - frac_x) * (1.0 - frac_y),
            frac_x * (1.0 - frac_y),
            (1.0 - frac_x) * frac_y,
            frac_x * frac_y,
        ]
    )
    return (texel_taps, weights)


def sample_matrix(texel_taps, weights, texel):
    positions = lax.broadcasted_iota(jnp.int32, (texel_taps.shape[1], texel), 1)
    matrix = jnp.zeros((texel_taps.shape[1], texel), jnp.float32)
    for number in range(4):
        matrix = matrix + jnp.where(
            texel_taps[number][:, None] == positions, weights[number][:, None], jnp.float32(0.0)
        )
    return matrix.astype(jnp.bfloat16)


def shifted(picture, shift_y, shift_x):
    height = picture.shape[1]
    width = picture.shape[2]
    padded_input = jnp.pad(picture, ((0, 0), (1, 1), (1, 1)))
    return padded_input[:, 1 + shift_y : 1 + shift_y + height, 1 + shift_x : 1 + shift_x + width]


def render_one(fetched, slot_row, cell_row, frac_row, conv_weight, cot_row):
    visible = fetched.shape[0]
    channels = fetched.shape[1]
    texel = fetched.shape[2]
    side = math.isqrt(texel)
    height = slot_row.shape[0]
    width = cell_row.shape[0] // height
    group_size = math.gcd(height, 16)
    group_count = height // group_size
    texel_taps, weights = taps_and_weights(cell_row, frac_row, side)
    taps_grouped = texel_taps.reshape(4, group_count, group_size * width).transpose(1, 0, 2)
    weights_grouped = weights.reshape(4, group_count, group_size * width).transpose(1, 0, 2)
    slots_grouped = slot_row.reshape(group_count, group_size)

    def forward(inputs):
        taps_part, weights_part, slots_part = inputs
        texture_lookup = sample_matrix(taps_part, weights_part, texel).reshape(
            group_size, width, texel
        )
        selected_entries = jnp.take(fetched, slots_part, axis=0)
        feature_maps = jnp.einsum(
            "qfm,qzm->qfz", selected_entries, texture_lookup, preferred_element_type=jnp.float32
        )
        return feature_maps.astype(jnp.bfloat16)

    grouped_features = lax.map(forward, (taps_grouped, weights_grouped, slots_grouped))
    feature_maps = grouped_features.transpose(2, 0, 1, 3).reshape(channels, height, width)
    offsets = [(shift_y, shift_x) for shift_y in (-1, 0, 1) for shift_x in (-1, 0, 1)]
    columns = jnp.concatenate(
        [shifted(feature_maps, shift_y, shift_x) for shift_y, shift_x in offsets], axis=0
    )
    columns = columns.reshape(9 * channels, height * width)
    preact = jnp.dot(conv_weight, columns, preferred_element_type=jnp.float32)
    sigmoid_pre = jax.nn.sigmoid(preact)
    rendered = (preact * sigmoid_pre).astype(jnp.bfloat16)
    pre_grad = (
        cot_row.astype(jnp.float32) * sigmoid_pre * (1.0 + preact * (1.0 - sigmoid_pre))
    ).astype(jnp.bfloat16)
    weight_local = jnp.einsum("op,kp->ok", pre_grad, columns, preferred_element_type=jnp.float32)
    col_grad = jnp.einsum("ok,op->kp", conv_weight, pre_grad, preferred_element_type=jnp.float32)
    col_grad = col_grad.reshape(9, channels, height, width)
    feat_grad = jnp.zeros((channels, height, width), jnp.float32)
    for number in range(9):
        shift_y, shift_x = offsets[number]
        feat_grad = feat_grad + shifted(col_grad[number], -shift_y, -shift_x)
    feat_grad = feat_grad.astype(jnp.bfloat16)
    grad_grouped = feat_grad.reshape(channels, group_count, group_size, width).transpose(1, 2, 0, 3)
    slot_numbers = jnp.arange(visible, dtype=jnp.int32)

    def backward(totals, inputs):
        taps_part, weights_part, slots_part, gradient_portion = inputs
        texture_lookup = sample_matrix(taps_part, weights_part, texel).reshape(
            group_size, width, texel
        )
        texel_gradient = jnp.einsum(
            "rzs,rsu->rzu", gradient_portion, texture_lookup, preferred_element_type=jnp.float32
        )
        selector = (slots_part[:, None] == slot_numbers[None, :]).astype(jnp.float32)
        added = jnp.einsum("gv,gct->vct", selector, texel_gradient, precision=lax.Precision.HIGHEST)
        return (totals + added, None)

    start = jnp.zeros((visible, channels, texel), jnp.float32)
    slot_grad, unused = lax.scan(
        backward, start, (taps_grouped, weights_grouped, slots_grouped, grad_grouped)
    )
    return (rendered, slot_grad.reshape(visible, channels * texel), weight_local)


def render_flat(fetched, slot_row, lookup, conv_weight, cot_row):
    visible = fetched.shape[0]
    channels = fetched.shape[1]
    texel = fetched.shape[2]
    height = slot_row.shape[0]
    width = lookup.shape[1]
    selected_entries = jnp.take(fetched, slot_row, axis=0, mode="clip")
    feature_maps = jnp.einsum(
        "qfm,qzm->fqz", selected_entries, lookup, preferred_element_type=jnp.float32
    ).astype(jnp.bfloat16)
    offsets = [(shift_y, shift_x) for shift_y in (-1, 0, 1) for shift_x in (-1, 0, 1)]
    columns = jnp.concatenate(
        [shifted(feature_maps, shift_y, shift_x) for shift_y, shift_x in offsets], axis=0
    )
    columns = columns.reshape(9 * channels, height * width)
    preact = jnp.dot(conv_weight, columns, preferred_element_type=jnp.float32)
    sigmoid_pre = jax.nn.sigmoid(preact)
    rendered = (preact * sigmoid_pre).astype(jnp.bfloat16)
    pre_grad = (
        cot_row.astype(jnp.float32) * sigmoid_pre * (1.0 + preact * (1.0 - sigmoid_pre))
    ).astype(jnp.bfloat16)
    weight_local = jnp.einsum("op,kp->ok", pre_grad, columns, preferred_element_type=jnp.float32)
    col_grad = jnp.einsum("ok,op->kp", conv_weight, pre_grad, preferred_element_type=jnp.float32)
    col_grad = col_grad.reshape(9, channels, height, width)
    feat_grad = jnp.zeros((channels, height, width), jnp.float32)
    for number in range(9):
        shift_y, shift_x = offsets[number]
        feat_grad = feat_grad + shifted(col_grad[number], -shift_y, -shift_x)
    feat_grad = feat_grad.astype(jnp.bfloat16)
    texel_gradient = jnp.einsum(
        "zrs,rsu->rzu", feat_grad, lookup, preferred_element_type=jnp.float32
    )
    slot_numbers = jnp.arange(visible, dtype=jnp.int32)
    selector = (slot_row[:, None] == slot_numbers[None, :]).astype(jnp.float32)
    blocks = texel // LANE // 2
    slot_grad = jnp.einsum(
        "gv,gcbt->cbvt",
        selector,
        texel_gradient.reshape(height, channels, blocks, texel // blocks),
        precision=lax.Precision.HIGHEST,
    )
    return (rendered, slot_grad, weight_local)


def per_device(texture, requests, block_slot, texel_cell, uv_frac, conv_weight, cotangent):
    owners = lax.axis_size("tex")
    frame_count = lax.axis_size("frames")
    tile_count = texture.shape[0]
    tile_width = texture.shape[1]
    texel = tile_width // CH
    height = block_slot.shape[1]
    texel_taps, weights = taps_and_weights(texel_cell[0], uv_frac[0], math.isqrt(texel))
    lookup = sample_matrix(texel_taps, weights, texel).reshape(height, -1, texel)
    lookup = lax.optimization_barrier(lookup)
    wanted_ids = requests.reshape(owners, -1)
    wanted = lax.all_to_all(wanted_ids, "tex", split_axis=0, concat_axis=0, tiled=True)
    per_owner = wanted.shape[1]
    visible = owners * per_owner
    served = jnp.take(
        texture.reshape(tile_count, CH, texel), wanted.reshape(-1), axis=0, mode="clip"
    ).reshape(owners, per_owner * CH, texel)
    fetched = lax.all_to_all(served, "tex", split_axis=0, concat_axis=0, tiled=True)
    fetched = fetched.reshape(visible, CH, texel)
    rendered, slot_grad, weight_local = render_flat(
        fetched, block_slot[0], lookup, conv_weight, cotangent[0]
    )
    columns = tile_width // frame_count
    weight_size = weight_local.size
    chunk = -(-weight_size // frame_count)
    request_count = requests.shape[1]
    weight_rows = jnp.pad(weight_local.reshape(-1), (0, chunk * frame_count - weight_size))
    weight_rows = weight_rows.reshape(frame_count, chunk)
    weight_high = weight_rows.astype(jnp.bfloat16)
    weight_low = (weight_rows - weight_high.astype(jnp.float32)).astype(jnp.bfloat16)
    extra = -(-(2 * chunk + request_count) // columns)
    side_row = jnp.concatenate(
        [
            weight_high,
            weight_low,
            jnp.broadcast_to(requests.astype(jnp.bfloat16), (frame_count, request_count)),
            jnp.zeros((frame_count, extra * columns - 2 * chunk - request_count), jnp.bfloat16),
        ],
        axis=1,
    ).reshape(frame_count, extra * columns // LANE, LANE)
    spread = slot_grad.reshape(frame_count, visible, columns)
    spread = spread.astype(jnp.bfloat16).reshape(frame_count, visible * columns // LANE, LANE)
    spread = jnp.concatenate([spread, side_row], axis=1)
    gathered = lax.all_to_all(spread, "frames", split_axis=0, concat_axis=0, tiled=True)
    grad_rows = visible * columns // LANE
    side = gathered[:, grad_rows:].reshape(frame_count, extra * columns).astype(jnp.float32)
    frame_weight = jnp.sum(side[:, :chunk] + side[:, chunk : 2 * chunk], axis=0)
    senders = side[:, 2 * chunk : 2 * chunk + request_count].astype(jnp.int32)
    senders = senders.reshape(frame_count, owners, per_owner)
    gathered = gathered[:, :grad_rows].astype(jnp.float32)
    gathered = gathered.reshape(frame_count, owners, per_owner, columns)
    tile_numbers = jnp.arange(tile_count, dtype=jnp.int32)
    selector = (senders[None] == tile_numbers[:, None, None, None]).astype(jnp.float32)
    partial = jnp.einsum(
        "qfoj,fojc->oqc", selector, gathered, precision=lax.Precision.HIGHEST
    )
    weight_high = frame_weight.astype(jnp.bfloat16)
    weight_low = (frame_weight - weight_high.astype(jnp.float32)).astype(jnp.bfloat16)
    weight_tail = -(-(2 * chunk) // columns) * columns
    weight_block = jnp.pad(
        jnp.concatenate([weight_high, weight_low]), (0, weight_tail - 2 * chunk)
    ).reshape(1, -1, LANE)
    partial = jnp.concatenate(
        [
            partial.astype(jnp.bfloat16).reshape(owners, tile_count * columns // LANE, LANE),
            jnp.broadcast_to(weight_block, (owners,) + weight_block.shape[1:]),
        ],
        axis=1,
    )
    received = lax.all_to_all(partial, "tex", 0, 0, tiled=True).astype(jnp.float32)
    collected = jnp.sum(received, axis=0)
    tile_rows = tile_count * columns // LANE
    texture_grad = collected[:tile_rows].reshape(tile_count, columns)
    weight_pair = collected[tile_rows:].reshape(-1)
    chunk_total = weight_pair[:chunk] + weight_pair[chunk : 2 * chunk]
    shared = lax.all_to_all(
        jnp.broadcast_to(chunk_total[None], (frame_count, chunk)), "frames", 0, 0, tiled=True
    )
    norm_scale = 1.0 / math.sqrt(frame_count * owners * cotangent.shape[2])
    weight_grad = shared.reshape(-1)[:weight_size].reshape(weight_local.shape) * norm_scale
    return (rendered[None], texture_grad, weight_grad)


def solution(mesh):
    placed = (
        P("tex", None),
        P(("frames", "tex"), None),
        P(("frames", "tex"), None),
        P(("frames", "tex"), None),
        P(("frames", "tex"), None, None),
        P(),
        P(("frames", "tex"), None, None),
    )
    return jax.shard_map(
        per_device,
        mesh=mesh,
        in_specs=placed,
        out_specs=(P(("frames", "tex"), None, None), P("tex", "frames"), P()),
        check_vma=False,
    )
```

```python
import math

import jax
import jax.numpy as jnp
from jax import lax
from jax.sharding import PartitionSpec as P

CH = 16
LANE = 128


def taps_and_weights(cell_row, frac_row, side):
    column = cell_row % (side - 1)
    row_index = cell_row // (side - 1)
    corner = row_index * side + column
    texel_taps = jnp.stack([corner, corner + 1, corner + side, corner + side + 1])
    frac_x = frac_row[0]
    frac_y = frac_row[1]
    weights = jnp.stack(
        [
            (1.0 - frac_x) * (1.0 - frac_y),
            frac_x * (1.0 - frac_y),
            (1.0 - frac_x) * frac_y,
            frac_x * frac_y,
        ]
    )
    return (texel_taps, weights)


def sample_matrix(texel_taps, weights, texel):
    positions = lax.broadcasted_iota(jnp.int32, (texel_taps.shape[1], texel), 1)
    matrix = jnp.zeros((texel_taps.shape[1], texel), jnp.float32)
    for number in range(4):
        matrix = matrix + jnp.where(
            texel_taps[number][:, None] == positions, weights[number][:, None], jnp.float32(0.0)
        )
    return matrix.astype(jnp.bfloat16)


def shifted(picture, shift_y, shift_x):
    height = picture.shape[1]
    width = picture.shape[2]
    padded_input = jnp.pad(picture, ((0, 0), (1, 1), (1, 1)))
    return padded_input[:, 1 + shift_y : 1 + shift_y + height, 1 + shift_x : 1 + shift_x + width]


def render_one(fetched, slot_row, cell_row, frac_row, conv_weight, cot_row):
    visible = fetched.shape[0]
    channels = fetched.shape[1]
    texel = fetched.shape[2]
    side = math.isqrt(texel)
    height = slot_row.shape[0]
    width = cell_row.shape[0] // height
    group_size = math.gcd(height, 16)
    group_count = height // group_size
    texel_taps, weights = taps_and_weights(cell_row, frac_row, side)
    taps_grouped = texel_taps.reshape(4, group_count, group_size * width).transpose(1, 0, 2)
    weights_grouped = weights.reshape(4, group_count, group_size * width).transpose(1, 0, 2)
    slots_grouped = slot_row.reshape(group_count, group_size)

    def forward(inputs):
        taps_part, weights_part, slots_part = inputs
        texture_lookup = sample_matrix(taps_part, weights_part, texel).reshape(
            group_size, width, texel
        )
        selected_entries = jnp.take(fetched, slots_part, axis=0)
        feature_maps = jnp.einsum(
            "qfm,qzm->qfz", selected_entries, texture_lookup, preferred_element_type=jnp.float32
        )
        return feature_maps.astype(jnp.bfloat16)

    grouped_features = lax.map(forward, (taps_grouped, weights_grouped, slots_grouped))
    feature_maps = grouped_features.transpose(2, 0, 1, 3).reshape(channels, height, width)
    offsets = [(shift_y, shift_x) for shift_y in (-1, 0, 1) for shift_x in (-1, 0, 1)]
    columns = jnp.concatenate(
        [shifted(feature_maps, shift_y, shift_x) for shift_y, shift_x in offsets], axis=0
    )
    columns = columns.reshape(9 * channels, height * width)
    preact = jnp.dot(conv_weight, columns, preferred_element_type=jnp.float32)
    sigmoid_pre = jax.nn.sigmoid(preact)
    rendered = (preact * sigmoid_pre).astype(jnp.bfloat16)
    pre_grad = (
        cot_row.astype(jnp.float32) * sigmoid_pre * (1.0 + preact * (1.0 - sigmoid_pre))
    ).astype(jnp.bfloat16)
    weight_local = jnp.einsum("op,kp->ok", pre_grad, columns, preferred_element_type=jnp.float32)
    col_grad = jnp.einsum("ok,op->kp", conv_weight, pre_grad, preferred_element_type=jnp.float32)
    col_grad = col_grad.reshape(9, channels, height, width)
    feat_grad = jnp.zeros((channels, height, width), jnp.float32)
    for number in range(9):
        shift_y, shift_x = offsets[number]
        feat_grad = feat_grad + shifted(col_grad[number], -shift_y, -shift_x)
    feat_grad = feat_grad.astype(jnp.bfloat16)
    grad_grouped = feat_grad.reshape(channels, group_count, group_size, width).transpose(1, 2, 0, 3)
    slot_numbers = jnp.arange(visible, dtype=jnp.int32)

    def backward(totals, inputs):
        taps_part, weights_part, slots_part, gradient_portion = inputs
        texture_lookup = sample_matrix(taps_part, weights_part, texel).reshape(
            group_size, width, texel
        )
        texel_gradient = jnp.einsum(
            "rzs,rsu->rzu", gradient_portion, texture_lookup, preferred_element_type=jnp.float32
        )
        selector = (slots_part[:, None] == slot_numbers[None, :]).astype(jnp.float32)
        added = jnp.einsum("gv,gct->vct", selector, texel_gradient, precision=lax.Precision.HIGHEST)
        return (totals + added, None)

    start = jnp.zeros((visible, channels, texel), jnp.float32)
    slot_grad, unused = lax.scan(
        backward, start, (taps_grouped, weights_grouped, slots_grouped, grad_grouped)
    )
    return (rendered, slot_grad.reshape(visible, channels * texel), weight_local)


def render_flat(fetched, slot_row, lookup, conv_weight, cot_row):
    visible = fetched.shape[0]
    channels = fetched.shape[1]
    texel = fetched.shape[2]
    height = slot_row.shape[0]
    width = lookup.shape[1]
    selected_entries = jnp.take(fetched, slot_row, axis=0, mode="clip")
    feature_maps = jnp.einsum(
        "qfm,qzm->qfz", selected_entries, lookup, preferred_element_type=jnp.float32
    ).astype(jnp.bfloat16)
    feature_maps = feature_maps.transpose(1, 0, 2)
    offsets = [(shift_y, shift_x) for shift_y in (-1, 0, 1) for shift_x in (-1, 0, 1)]
    columns = jnp.concatenate(
        [shifted(feature_maps, shift_y, shift_x) for shift_y, shift_x in offsets], axis=0
    )
    columns = columns.reshape(9 * channels, height * width)
    preact = jnp.dot(conv_weight, columns, preferred_element_type=jnp.float32)
    sigmoid_pre = jax.nn.sigmoid(preact)
    rendered = (preact * sigmoid_pre).astype(jnp.bfloat16)
    pre_grad = (
        cot_row.astype(jnp.float32) * sigmoid_pre * (1.0 + preact * (1.0 - sigmoid_pre))
    ).astype(jnp.bfloat16)
    weight_local = jnp.einsum("op,kp->ok", pre_grad, columns, preferred_element_type=jnp.float32)
    col_grad = jnp.einsum("ok,op->kp", conv_weight, pre_grad, preferred_element_type=jnp.float32)
    col_grad = col_grad.reshape(9, channels, height, width)
    feat_grad = jnp.zeros((channels, height, width), jnp.float32)
    for number in range(9):
        shift_y, shift_x = offsets[number]
        feat_grad = feat_grad + shifted(col_grad[number], -shift_y, -shift_x)
    feat_grad = feat_grad.astype(jnp.bfloat16)
    texel_gradient = jnp.einsum(
        "zrs,rsu->rzu", feat_grad, lookup, preferred_element_type=jnp.float32
    )
    slot_numbers = jnp.arange(visible, dtype=jnp.int32)
    selector = (slot_row[:, None] == slot_numbers[None, :]).astype(jnp.float32)
    slot_grad = jnp.einsum(
        "gv,gct->vct", selector, texel_gradient, precision=lax.Precision.HIGHEST
    )
    return (rendered, slot_grad.reshape(visible, channels * texel), weight_local)


def per_device(texture, requests, block_slot, texel_cell, uv_frac, conv_weight, cotangent):
    owners = lax.axis_size("tex")
    frame_count = lax.axis_size("frames")
    tile_count = texture.shape[0]
    tile_width = texture.shape[1]
    texel = tile_width // CH
    height = block_slot.shape[1]
    texel_taps, weights = taps_and_weights(texel_cell[0], uv_frac[0], math.isqrt(texel))
    lookup = sample_matrix(texel_taps, weights, texel).reshape(height, -1, texel)
    lookup = lax.optimization_barrier(lookup)
    wanted_ids = requests.reshape(owners, -1)
    wanted = lax.all_to_all(wanted_ids, "tex", split_axis=0, concat_axis=0, tiled=True)
    per_owner = wanted.shape[1]
    visible = owners * per_owner
    served = jnp.take(
        texture.reshape(tile_count, CH, texel), wanted.reshape(-1), axis=0, mode="clip"
    ).reshape(owners, per_owner * CH, texel)
    fetched = lax.all_to_all(served, "tex", split_axis=0, concat_axis=0, tiled=True)
    fetched = fetched.reshape(visible, CH, texel)
    rendered, slot_grad, weight_local = render_flat(
        fetched, block_slot[0], lookup, conv_weight, cotangent[0]
    )
    columns = tile_width // frame_count
    weight_size = weight_local.size
    chunk = -(-weight_size // frame_count)
    request_count = requests.shape[1]
    weight_rows = jnp.pad(weight_local.reshape(-1), (0, chunk * frame_count - weight_size))
    weight_rows = weight_rows.reshape(frame_count, chunk)
    weight_high = weight_rows.astype(jnp.bfloat16)
    weight_low = (weight_rows - weight_high.astype(jnp.float32)).astype(jnp.bfloat16)
    extra = -(-(2 * chunk + request_count) // columns)
    side_row = jnp.concatenate(
        [
            weight_high,
            weight_low,
            jnp.broadcast_to(requests.astype(jnp.bfloat16), (frame_count, request_count)),
            jnp.zeros((frame_count, extra * columns - 2 * chunk - request_count), jnp.bfloat16),
        ],
        axis=1,
    ).reshape(frame_count, extra * columns // LANE, LANE)
    spread = slot_grad.reshape(visible, frame_count, columns).transpose(1, 0, 2)
    spread = spread.astype(jnp.bfloat16).reshape(frame_count, visible * columns // LANE, LANE)
    spread = jnp.concatenate([spread, side_row], axis=1)
    gathered = lax.all_to_all(spread, "frames", split_axis=0, concat_axis=0, tiled=True)
    grad_rows = visible * columns // LANE
    side = gathered[:, grad_rows:].reshape(frame_count, extra * columns).astype(jnp.float32)
    frame_weight = jnp.sum(side[:, :chunk] + side[:, chunk : 2 * chunk], axis=0)
    senders = side[:, 2 * chunk : 2 * chunk + request_count].astype(jnp.int32)
    senders = senders.reshape(frame_count, owners, per_owner)
    gathered = gathered[:, :grad_rows].astype(jnp.float32)
    gathered = gathered.reshape(frame_count, owners, per_owner, columns)
    tile_numbers = jnp.arange(tile_count, dtype=jnp.int32)
    selector = (senders[None] == tile_numbers[:, None, None, None]).astype(jnp.float32)
    partial = jnp.einsum(
        "qfoj,fojc->oqc", selector, gathered, precision=lax.Precision.HIGHEST
    )
    weight_high = frame_weight.astype(jnp.bfloat16)
    weight_low = (frame_weight - weight_high.astype(jnp.float32)).astype(jnp.bfloat16)
    weight_tail = -(-(2 * chunk) // columns) * columns
    weight_block = jnp.pad(
        jnp.concatenate([weight_high, weight_low]), (0, weight_tail - 2 * chunk)
    ).reshape(1, -1, LANE)
    partial = jnp.concatenate(
        [
            partial.astype(jnp.bfloat16).reshape(owners, tile_count * columns // LANE, LANE),
            jnp.broadcast_to(weight_block, (owners,) + weight_block.shape[1:]),
        ],
        axis=1,
    )
    received = lax.all_to_all(partial, "tex", 0, 0, tiled=True).astype(jnp.float32)
    collected = jnp.sum(received, axis=0)
    tile_rows = tile_count * columns // LANE
    texture_grad = collected[:tile_rows].reshape(tile_count, columns)
    weight_pair = collected[tile_rows:].reshape(-1)
    chunk_total = weight_pair[:chunk] + weight_pair[chunk : 2 * chunk]
    shared = lax.all_to_all(
        jnp.broadcast_to(chunk_total[None], (frame_count, chunk)), "frames", 0, 0, tiled=True
    )
    norm_scale = 1.0 / math.sqrt(frame_count * owners * cotangent.shape[2])
    weight_grad = shared.reshape(-1)[:weight_size].reshape(weight_local.shape) * norm_scale
    return (rendered[None], texture_grad, weight_grad)


def solution(mesh):
    placed = (
        P("tex", None),
        P(("frames", "tex"), None),
        P(("frames", "tex"), None),
        P(("frames", "tex"), None),
        P(("frames", "tex"), None, None),
        P(),
        P(("frames", "tex"), None, None),
    )
    return jax.shard_map(
        per_device,
        mesh=mesh,
        in_specs=placed,
        out_specs=(P(("frames", "tex"), None, None), P("tex", "frames"), P()),
        check_vma=False,
    )
```

```python
import math

import jax
import jax.numpy as jnp
from jax import lax
from jax.sharding import PartitionSpec as P

CH = 16
LANE = 128


def taps_and_weights(cell_row, frac_row, side):
    column = cell_row % (side - 1)
    row_index = cell_row // (side - 1)
    corner = row_index * side + column
    texel_taps = jnp.stack([corner, corner + 1, corner + side, corner + side + 1])
    frac_x = frac_row[0]
    frac_y = frac_row[1]
    weights = jnp.stack(
        [
            (1.0 - frac_x) * (1.0 - frac_y),
            frac_x * (1.0 - frac_y),
            (1.0 - frac_x) * frac_y,
            frac_x * frac_y,
        ]
    )
    return (texel_taps, weights)


def sample_matrix(texel_taps, weights, texel):
    positions = lax.broadcasted_iota(jnp.int32, (texel_taps.shape[1], texel), 1)
    matrix = jnp.zeros((texel_taps.shape[1], texel), jnp.float32)
    for number in range(4):
        matrix = matrix + jnp.where(
            texel_taps[number][:, None] == positions, weights[number][:, None], jnp.float32(0.0)
        )
    return matrix.astype(jnp.bfloat16)


def shifted(picture, shift_y, shift_x):
    height = picture.shape[1]
    width = picture.shape[2]
    padded_input = jnp.pad(picture, ((0, 0), (1, 1), (1, 1)))
    return padded_input[:, 1 + shift_y : 1 + shift_y + height, 1 + shift_x : 1 + shift_x + width]


def render_one(fetched, slot_row, cell_row, frac_row, conv_weight, cot_row):
    visible = fetched.shape[0]
    channels = fetched.shape[1]
    texel = fetched.shape[2]
    side = math.isqrt(texel)
    height = slot_row.shape[0]
    width = cell_row.shape[0] // height
    group_size = math.gcd(height, 16)
    group_count = height // group_size
    texel_taps, weights = taps_and_weights(cell_row, frac_row, side)
    taps_grouped = texel_taps.reshape(4, group_count, group_size * width).transpose(1, 0, 2)
    weights_grouped = weights.reshape(4, group_count, group_size * width).transpose(1, 0, 2)
    slots_grouped = slot_row.reshape(group_count, group_size)

    def forward(inputs):
        taps_part, weights_part, slots_part = inputs
        texture_lookup = sample_matrix(taps_part, weights_part, texel).reshape(
            group_size, width, texel
        )
        selected_entries = jnp.take(fetched, slots_part, axis=0)
        feature_maps = jnp.einsum(
            "qfm,qzm->qfz", selected_entries, texture_lookup, preferred_element_type=jnp.float32
        )
        return feature_maps.astype(jnp.bfloat16)

    grouped_features = lax.map(forward, (taps_grouped, weights_grouped, slots_grouped))
    feature_maps = grouped_features.transpose(2, 0, 1, 3).reshape(channels, height, width)
    offsets = [(shift_y, shift_x) for shift_y in (-1, 0, 1) for shift_x in (-1, 0, 1)]
    columns = jnp.concatenate(
        [shifted(feature_maps, shift_y, shift_x) for shift_y, shift_x in offsets], axis=0
    )
    columns = columns.reshape(9 * channels, height * width)
    preact = jnp.dot(conv_weight, columns, preferred_element_type=jnp.float32)
    sigmoid_pre = jax.nn.sigmoid(preact)
    rendered = (preact * sigmoid_pre).astype(jnp.bfloat16)
    pre_grad = (
        cot_row.astype(jnp.float32) * sigmoid_pre * (1.0 + preact * (1.0 - sigmoid_pre))
    ).astype(jnp.bfloat16)
    weight_local = jnp.einsum("op,kp->ok", pre_grad, columns, preferred_element_type=jnp.float32)
    col_grad = jnp.einsum("ok,op->kp", conv_weight, pre_grad, preferred_element_type=jnp.float32)
    col_grad = col_grad.reshape(9, channels, height, width)
    feat_grad = jnp.zeros((channels, height, width), jnp.float32)
    for number in range(9):
        shift_y, shift_x = offsets[number]
        feat_grad = feat_grad + shifted(col_grad[number], -shift_y, -shift_x)
    feat_grad = feat_grad.astype(jnp.bfloat16)
    grad_grouped = feat_grad.reshape(channels, group_count, group_size, width).transpose(1, 2, 0, 3)
    slot_numbers = jnp.arange(visible, dtype=jnp.int32)

    def backward(totals, inputs):
        taps_part, weights_part, slots_part, gradient_portion = inputs
        texture_lookup = sample_matrix(taps_part, weights_part, texel).reshape(
            group_size, width, texel
        )
        texel_gradient = jnp.einsum(
            "rzs,rsu->rzu", gradient_portion, texture_lookup, preferred_element_type=jnp.float32
        )
        selector = (slots_part[:, None] == slot_numbers[None, :]).astype(jnp.float32)
        added = jnp.einsum("gv,gct->vct", selector, texel_gradient, precision=lax.Precision.HIGHEST)
        return (totals + added, None)

    start = jnp.zeros((visible, channels, texel), jnp.float32)
    slot_grad, unused = lax.scan(
        backward, start, (taps_grouped, weights_grouped, slots_grouped, grad_grouped)
    )
    return (rendered, slot_grad.reshape(visible, channels * texel), weight_local)


def render_flat(fetched, slot_row, lookup, conv_weight, cot_row):
    visible = fetched.shape[0]
    channels = fetched.shape[1]
    texel = fetched.shape[2]
    height = slot_row.shape[0]
    width = lookup.shape[1]
    selected_entries = jnp.take(fetched, slot_row, axis=0, mode="clip")
    feature_maps = jnp.einsum(
        "qfm,qzm->fqz", selected_entries, lookup, preferred_element_type=jnp.float32
    ).astype(jnp.bfloat16)
    offsets = [(shift_y, shift_x) for shift_y in (-1, 0, 1) for shift_x in (-1, 0, 1)]
    columns = jnp.concatenate(
        [shifted(feature_maps, shift_y, shift_x) for shift_y, shift_x in offsets], axis=0
    )
    columns = columns.reshape(9 * channels, height * width)
    preact = jnp.dot(conv_weight, columns, preferred_element_type=jnp.float32)
    sigmoid_pre = jax.nn.sigmoid(preact)
    rendered = (preact * sigmoid_pre).astype(jnp.bfloat16)
    pre_grad = (
        cot_row.astype(jnp.float32) * sigmoid_pre * (1.0 + preact * (1.0 - sigmoid_pre))
    ).astype(jnp.bfloat16)
    weight_local = jnp.einsum("op,kp->ok", pre_grad, columns, preferred_element_type=jnp.float32)
    col_grad = jnp.einsum("ok,op->kp", conv_weight, pre_grad, preferred_element_type=jnp.float32)
    col_grad = col_grad.reshape(9, channels, height, width)
    feat_grad = jnp.zeros((channels, height, width), jnp.float32)
    for number in range(9):
        shift_y, shift_x = offsets[number]
        feat_grad = feat_grad + shifted(col_grad[number], -shift_y, -shift_x)
    feat_grad = feat_grad.astype(jnp.bfloat16)
    texel_gradient = jnp.einsum(
        "zrs,rsu->rzu", feat_grad, lookup, preferred_element_type=jnp.float32
    )
    slot_numbers = jnp.arange(visible, dtype=jnp.int32)
    selector = (slot_row[:, None] == slot_numbers[None, :]).astype(jnp.float32)
    slot_grad = jnp.einsum(
        "gv,gct->vct", selector, texel_gradient, precision=lax.Precision.HIGHEST
    )
    return (rendered, slot_grad.reshape(visible, channels * texel), weight_local)


def per_device(texture, requests, block_slot, texel_cell, uv_frac, conv_weight, cotangent):
    owners = lax.axis_size("tex")
    frame_count = lax.axis_size("frames")
    tile_count = texture.shape[0]
    tile_width = texture.shape[1]
    texel = tile_width // CH
    height = block_slot.shape[1]
    texel_taps, weights = taps_and_weights(texel_cell[0], uv_frac[0], math.isqrt(texel))
    lookup = sample_matrix(texel_taps, weights, texel).reshape(height, -1, texel)
    lookup = lax.optimization_barrier(lookup)
    wanted_ids = requests.reshape(owners, -1)
    wanted = lax.all_to_all(wanted_ids, "tex", split_axis=0, concat_axis=0, tiled=True)
    per_owner = wanted.shape[1]
    visible = owners * per_owner
    served = jnp.take(
        texture.reshape(tile_count, CH, texel), wanted.reshape(-1), axis=0, mode="clip"
    ).reshape(owners, per_owner * CH, texel)
    fetched = lax.all_to_all(served, "tex", split_axis=0, concat_axis=0, tiled=True)
    fetched = fetched.reshape(visible, CH, texel)
    rendered, slot_grad, weight_local = render_flat(
        fetched, block_slot[0], lookup, conv_weight, cotangent[0]
    )
    columns = tile_width // frame_count
    weight_size = weight_local.size
    chunk = -(-weight_size // frame_count)
    request_count = requests.shape[1]
    weight_rows = jnp.pad(weight_local.reshape(-1), (0, chunk * frame_count - weight_size))
    weight_rows = weight_rows.reshape(frame_count, chunk)
    weight_high = weight_rows.astype(jnp.bfloat16)
    weight_low = (weight_rows - weight_high.astype(jnp.float32)).astype(jnp.bfloat16)
    extra = -(-(2 * chunk + request_count) // columns)
    side_row = jnp.concatenate(
        [
            weight_high,
            weight_low,
            jnp.broadcast_to(requests.astype(jnp.bfloat16), (frame_count, request_count)),
            jnp.zeros((frame_count, extra * columns - 2 * chunk - request_count), jnp.bfloat16),
        ],
        axis=1,
    ).reshape(frame_count, extra * columns // LANE, LANE)
    spread = slot_grad.reshape(visible, frame_count, columns).transpose(1, 0, 2)
    spread = spread.astype(jnp.bfloat16).reshape(frame_count, visible * columns // LANE, LANE)
    spread = jnp.concatenate([spread, side_row], axis=1)
    payload_rows = spread.shape[1]
    gathered = lax.all_to_all(
        spread.reshape(frame_count, -1), "frames", split_axis=0, concat_axis=0, tiled=True
    ).reshape(frame_count, payload_rows, LANE)
    grad_rows = visible * columns // LANE
    side = gathered[:, grad_rows:].reshape(frame_count, extra * columns).astype(jnp.float32)
    frame_weight = jnp.sum(side[:, :chunk] + side[:, chunk : 2 * chunk], axis=0)
    senders = side[:, 2 * chunk : 2 * chunk + request_count].astype(jnp.int32)
    senders = senders.reshape(frame_count, owners, per_owner)
    gathered = gathered[:, :grad_rows].astype(jnp.float32)
    gathered = gathered.reshape(frame_count, owners, per_owner, columns)
    tile_numbers = jnp.arange(tile_count, dtype=jnp.int32)
    selector = (senders[None] == tile_numbers[:, None, None, None]).astype(jnp.float32)
    partial = jnp.einsum(
        "qfoj,fojc->oqc", selector, gathered, precision=lax.Precision.HIGHEST
    )
    weight_high = frame_weight.astype(jnp.bfloat16)
    weight_low = (frame_weight - weight_high.astype(jnp.float32)).astype(jnp.bfloat16)
    weight_tail = -(-(2 * chunk) // columns) * columns
    weight_block = jnp.pad(
        jnp.concatenate([weight_high, weight_low]), (0, weight_tail - 2 * chunk)
    ).reshape(1, -1, LANE)
    partial = jnp.concatenate(
        [
            partial.astype(jnp.bfloat16).reshape(owners, tile_count * columns // LANE, LANE),
            jnp.broadcast_to(weight_block, (owners,) + weight_block.shape[1:]),
        ],
        axis=1,
    )
    received = lax.all_to_all(partial, "tex", 0, 0, tiled=True).astype(jnp.float32)
    collected = jnp.sum(received, axis=0)
    tile_rows = tile_count * columns // LANE
    texture_grad = collected[:tile_rows].reshape(tile_count, columns)
    weight_pair = collected[tile_rows:].reshape(-1)
    chunk_total = weight_pair[:chunk] + weight_pair[chunk : 2 * chunk]
    shared = lax.all_to_all(
        jnp.broadcast_to(chunk_total[None], (frame_count, chunk)), "frames", 0, 0, tiled=True
    )
    norm_scale = 1.0 / math.sqrt(frame_count * owners * cotangent.shape[2])
    weight_grad = shared.reshape(-1)[:weight_size].reshape(weight_local.shape) * norm_scale
    return (rendered[None], texture_grad, weight_grad)


def solution(mesh):
    placed = (
        P("tex", None),
        P(("frames", "tex"), None),
        P(("frames", "tex"), None),
        P(("frames", "tex"), None),
        P(("frames", "tex"), None, None),
        P(),
        P(("frames", "tex"), None, None),
    )
    return jax.shard_map(
        per_device,
        mesh=mesh,
        in_specs=placed,
        out_specs=(P(("frames", "tex"), None, None), P("tex", "frames"), P()),
        check_vma=False,
    )
```
